512 devices in a mesh: rows: 128 (over z, y, core), dp: 4 (over x).
Axes of the slice: x: 4, y: 4, z: 16, core: 2. Of those that a mesh axis runs over, the one named last changes fastest.
Arguments:
- tokens: bfloat16 [262144, 512], P(('rows', 'dp')), may hold values from -24 to 24
- out_grad: bfloat16 [262144, 512], P(('rows', 'dp')), may hold values from -24 to 24
- seq_lengths: int32 [512, 4], P(('rows', 'dp')), may hold values from 1 to 256, 512 in all within a row
- owners: int32 [262144, 1], P(('rows', 'dp')), may hold values from 0 to 127; in each aligned block of 512 rows (0 to 511, 512 to 1023, ...) at most 16 rows name the same one
- slots: int32 [262144], P(('rows', 'dp')), may hold values from 0 to 127
- w_in: bfloat16 [512, 1024], replicated, may hold values from -0.25 to 0.25
- w_out: bfloat16 [512, 256], replicated, may hold values from -0.375 to 0.375
- emb_rows: float32 [16384, 512], P('rows'), may hold values from -0.6 to 0.6
- emb_mom: float32 [16384, 512], P('rows'), may hold values from -0.6 to 0.6
- emb_var: float32 [16384], P('rows'), may hold values from 0.01 to 0.1
Outputs:
- new_rows: float32 [16384, 512], P('rows')
- new_mom: float32 [16384, 512], P('rows')
- new_var: float32 [16384], P('rows')
- w_in_grad: float32 [512, 1024], P('rows')
- w_out_grad: float32 [512, 256], P('rows')
The draws below stay inside these ranges and needn't reach their ends.
Inputs may be any that keep to these rules, and one draw needn't show every extreme that they name: `seq_lengths`: each row sums to 512; its largest entry is exactly 256. `owners`: among the 512 tokens of one device at most 16 name the same owner; some device reaches 16.
All inputs are finite; a program needn't handle non-finite values.
Results may differ from the reference program's by a relative error of at most 0.015.
Values may be sent and summed in bfloat16 or wider, within the bound.
No kernel may reach another device: no remote copies, remote signals or barrier semaphores. Data moves between devices by JAX's collectives and lax.ppermute only.
A program may use at most 64 MiB of HBM per device.

```python
import math
import jax
import jax.numpy as jnp
import numpy as np
from jax import lax

D = 512
HEADS = 4
HEAD_DIM = 64
HW = 256
TOK_DEV = 512
NSEQ = 4
MAXLEN = 256
SLOTS = 128
CAP = 16
TOKENS = 262144
TABLE = 16384
N_ROWS = 128
DEVICES = 512


def touch_ends(array, own_key, low, largest):
    shape = array.shape
    spot = [jax.random.randint(jax.random.fold_in(own_key, axis), (), 0, shape[axis]) for axis in range(len(shape))]
    array = array.at[tuple(spot)].set(low)
    longest = shape.index(max(shape))
    spot[longest] = (spot[longest] + 1) % shape[longest]
    return array.at[tuple(spot)].set(largest)


def with_spikes(drawn, key, source, target, blocks, factor):
    owner, partner = [(jnp.arange(drawn.shape[dim]) // (drawn.shape[dim] // blocks)).reshape([-1 if axis == dim else 1 for axis in range(drawn.ndim)]) for dim in (source, target)]
    chosen = jax.random.permutation(key, blocks)[partner]
    strong = (owner == chosen) | (owner == (partner + blocks // 2) % blocks)
    return jnp.where(strong, factor * drawn, drawn)


def block_levels(own_key, shape, cuts, low, largest):
    loudness, own = 1.0, jax.random.fold_in(own_key, 6)
    for dim, shards_of in cuts:
        heights = jnp.exp(jax.random.uniform(jax.random.fold_in(own, dim), (shards_of,), jnp.float32, low / len(cuts), largest / len(cuts)))
        loudness = loudness * jnp.repeat(heights, shape[dim] // shards_of).reshape([-1 if axis == dim else 1 for axis in range(len(shape))])
    return loudness


def rank_table(number_of, slope):
    loads = [(1 << 20) // math.isqrt(rank ** slope) + 1 for rank in range(1, number_of + 1)]
    scale = 1 + sum(loads) // (1 << 30)
    return np.cumsum(np.array([max(1, weight // scale) for weight in loads]))


def ranked(rng, shape, amount, skew):
    table = rank_table(amount, skew)
    lot = jax.random.randint(jax.random.fold_in(rng, 1), shape, 0, int(table[amount - 1]))
    standing = jnp.searchsorted(jnp.asarray(table, jnp.int32), lot, side="right")
    return jax.random.permutation(jax.random.fold_in(rng, 2), amount)[standing].astype(jnp.int32)


def profile(amount, total, reach, lean):
    loads = [(1 << 20) // math.isqrt(standing ** lean) + 1 for standing in range(2, amount + 1)]
    surplus, given = total - reach - (amount - 1), [1] * (amount - 1)
    while surplus > 0:
        free = [i for i in range(amount - 1) if given[i] < reach]
        pool, left = sum([loads[i] for i in free]), surplus
        for i in free:
            extra = min(reach - given[i], max(1, left * loads[i] // pool), surplus)
            given[i] = given[i] + extra
            surplus = surplus - extra
    return np.array([reach] + given)


def ragged_sizes(key, count, total, bound, slope):
    if count == 2:
        one = jax.random.randint(key, (), max(1, total - bound), min(bound, total - 1) + 1)
        return jnp.stack([one, total - one])
    sizes = jnp.asarray(profile(count, total, bound, slope), jnp.int32)
    pairs = (count - 1) // 2
    source_of, taker = sizes[1:1 + 2 * pairs:2], sizes[2:2 + 2 * pairs:2]
    margin = jnp.minimum(source_of - 1, bound - taker)
    moved = jax.random.randint(jax.random.fold_in(key, 1), (pairs,), 0, 1 << 20) % (margin + 1)
    sizes = sizes.at[1:1 + 2 * pairs:2].set(source_of - moved).at[2:2 + 2 * pairs:2].set(taker + moved)
    return sizes[jax.random.permutation(jax.random.fold_in(key, 2), count)]


def routed_block(own_key, own, number, rows, number_of, top, most, skew):
    order = jax.random.permutation(own_key, number_of)
    heavy_load, usual = portions_of(number_of, rows * top, most, skew, True), portions_of(number_of, rows * top, most, skew, False)
    places = jnp.arange(number_of)

    def named(sizes, rotation):
        used = int((sizes > 0).sum())
        fixed = max(1, used // 4)
        shifted = fixed + (places - fixed + rotation * (used - fixed)) % max(1, number_of - fixed)
        return jnp.zeros((number_of,), jnp.int32).at[order[jnp.where(places < fixed, places, shifted)]].set(jnp.asarray(sizes, jnp.int32))

    sizes = jnp.where(number % 4 == 0, named(heavy_load, number // 4), named(usual, number - number // 4 - 1))
    mixed = jax.random.permutation(jax.random.fold_in(own, 3), number_of)
    donor, sink = mixed[0:number_of // 2 * 2:2], mixed[1:number_of // 2 * 2:2]
    margin = jnp.minimum(sizes[donor] - 1, most - sizes[sink]) // 2
    margin = jnp.where((donor == order[0]) | (sink == order[0]) | (sizes[sink] == 0), 0, jnp.maximum(margin, 0))
    shifted = jax.random.randint(jax.random.fold_in(own, 4), (number_of // 2,), 0, 1 << 20) % (margin + 1)
    sizes = sizes.at[donor].add(-shifted).at[sink].add(shifted)
    labels = jnp.searchsorted(jnp.cumsum(sizes), jnp.arange(rows * top), side="right").astype(jnp.int32)
    listing = labels.reshape(top, rows).T
    listing = listing[jax.random.permutation(jax.random.fold_in(own, 1), rows)]
    rotation = jax.random.randint(jax.random.fold_in(own, 2), (rows, 1), 0, top)
    return jnp.take_along_axis(listing, (jnp.arange(top)[None, :] + rotation) % top, axis=1)


def portions_of(number_of, total, bound, skew, full):
    weights = [(1 << 20) // math.isqrt(rank ** skew) + 1 for rank in range(1, number_of + 1)]
    largest = bound if full else min(bound, max(-(-total // number_of), total * weights[0] // sum(weights)))
    least = 1 if total - largest >= number_of - 1 else 0
    holding, surplus = [largest] + [least] * (number_of - 1), total - largest - least * (number_of - 1)
    while surplus > 0:
        movable = [i for i in range(1, number_of) if holding[i] < largest] or [i for i in range(1, number_of) if holding[i] < bound]
        pool, left = sum([weights[i] for i in movable]), surplus
        for i in movable:
            addition = min(bound - holding[i], max(1, left * weights[i] // pool), surplus)
            holding[i] = holding[i] + addition
            surplus = surplus - addition
    return np.array(holding)


def scatter_about(own_key, shape, deviation, bound, pieces=(), kind=jnp.bfloat16):
    factor_of = block_levels(own_key, shape, pieces, -0.22, 0.18) if pieces else 1.0
    entries = jax.random.normal(own_key, shape, jnp.float32) * deviation * factor_of
    return jnp.minimum(jnp.maximum(entries, -bound), bound).astype(kind)


def gaussian_with(stream_key, shape, deviation, most, pieces, heavy, kind=jnp.bfloat16):
    result = deviation * jax.random.normal(stream_key, shape, jnp.float32)
    if pieces:
        result = result * block_levels(stream_key, shape, pieces, -0.22, 0.18)
    return jnp.clip(with_spikes(result, jax.random.fold_in(stream_key, 3), *heavy), -most, most).astype(kind)


def setup_inputs(seed: int = 0) -> dict:
    key_list = jax.random.split(jax.random.key(seed), 11)
    tokens = gaussian_with(key_list[0], (TOKENS, D), 1.0, 24.0, ((0, 512),), (0, 1, 512, 6.0))
    out_grad = gaussian_with(key_list[1], (TOKENS, D), 1.0, 24.0, ((0, 512),), (0, 1, 512, 6.0))
    seq_lengths = jax.vmap(lambda own: ragged_sizes(own, NSEQ, TOK_DEV, MAXLEN, 2))(jax.random.split(key_list[2], DEVICES)).reshape((DEVICES, NSEQ)).astype(jnp.int32)
    owners_keys = jax.random.split(jax.random.fold_in(key_list[3], 1), TOKENS // TOK_DEV)
    owners_turns = jax.random.permutation(jax.random.fold_in(key_list[3], 3), TOKENS // TOK_DEV)
    owners = jax.vmap(lambda own, number: routed_block(jax.random.fold_in(key_list[3], 2), own, number, TOK_DEV, N_ROWS, 1, CAP, 2))(owners_keys, owners_turns).reshape((TOKENS, 1))
    slots = touch_ends(ranked(key_list[4], (TOKENS,), SLOTS, 3), jax.random.fold_in(key_list[4], 3), 0, SLOTS - 1).astype(jnp.int32)
    w_in = scatter_about(key_list[5], (D, 4 * HW), D ** -0.5, 0.25)
    w_out = scatter_about(key_list[6], (D, HW), HW ** -0.5, 0.375)
    emb_rows = scatter_about(key_list[7], (TABLE, D), 0.1, 0.6, ((0, 128),), jnp.float32)
    emb_mom = scatter_about(key_list[8], (TABLE, D), 0.1, 0.6, ((0, 128),), jnp.float32)
    emb_var = jnp.clip(jnp.exp(math.log(0.1) - 2.3025851 * jax.random.uniform(key_list[9], (TABLE,), jnp.float32) ** block_levels(key_list[9], (TABLE,), ((0, 128),), -0.2, 0.2)), 0.01, 0.1)
    return dict(tokens=tokens, out_grad=out_grad, seq_lengths=seq_lengths, owners=owners, slots=slots, w_in=w_in, w_out=w_out, emb_rows=emb_rows, emb_mom=emb_mom, emb_var=emb_var)


norm_eps = 1e-06
beta_one = 0.9
beta_two = 0.99
learn_rate = 0.05
adam_eps = 1e-08
bias_one = 1.0 - 0.9 ** 10
bias_two = 1.0 - 0.99 ** 10

def layer_norm(values):
    average = lax.optimization_barrier(jnp.mean(values, axis=-1, keepdims=True))
    centered = values - average
    spread = lax.optimization_barrier(jnp.mean(centered * centered, axis=-1, keepdims=True))
    return centered * lax.rsqrt(spread + norm_eps)

def allowed_mask(lengths, tok_count):
    ends = jnp.cumsum(lengths.astype(jnp.int32))
    position = jnp.arange(tok_count, dtype=jnp.int32)
    segment = lax.optimization_barrier(jnp.sum((position[:, None] >= ends[None, :]).astype(jnp.int32), axis=1))
    same = segment[:, None] == segment[None, :]
    causal = position[None, :] <= position[:, None]
    return (same & causal).astype(jnp.float32)

def core(pre, allowed):
    tok_count = pre.shape[0]
    proj = jax.nn.silu(pre).astype(jnp.bfloat16)
    upart, vpart, qpart, kpart = jnp.split(proj, 4, axis=1)
    queries = qpart.reshape(tok_count, HEADS, HEAD_DIM).astype(jnp.float32)
    keys_part = kpart.reshape(tok_count, HEADS, HEAD_DIM).astype(jnp.float32)
    values_part = vpart.reshape(tok_count, HEADS, HEAD_DIM).astype(jnp.float32)
    scores = jnp.einsum('thd,shd->hts', queries, keys_part) * HEAD_DIM ** (-0.5)
    weights = (jax.nn.silu(scores) * allowed[None] / MAXLEN).astype(jnp.bfloat16)
    attn = jnp.einsum('hts,shd->thd', weights.astype(jnp.float32), values_part).reshape(tok_count, HW)
    return (layer_norm(attn) * upart.astype(jnp.float32)).astype(jnp.bfloat16)

def device_grads(x_part, grad_part, lengths, w_in, w_out):
    allowed = allowed_mask(lengths, x_part.shape[0])
    normed_exact, norm_back = jax.vjp(layer_norm, x_part.astype(jnp.float32))
    normed = normed_exact.astype(jnp.bfloat16)
    pre = jnp.dot(normed, w_in, preferred_element_type=jnp.float32)
    y_out, core_back = jax.vjp(lambda inner: core(inner, allowed), pre)
    y_grad = jnp.dot(grad_part, w_out, preferred_element_type=jnp.float32).astype(jnp.bfloat16)
    pre_grad = core_back(y_grad)[0]
    pre_grad_b = pre_grad.astype(jnp.bfloat16)
    contract = (((0,), (0,)), ((), ()))
    w_in_term = lax.dot_general(normed, pre_grad_b, contract, preferred_element_type=jnp.float32)
    w_out_term = lax.dot_general(grad_part, y_out, contract, preferred_element_type=jnp.float32)
    normed_grad = lax.dot_general(pre_grad_b, w_in, (((1,), (1,)), ((), ())), preferred_element_type=jnp.float32)
    x_grad = norm_back(normed_grad)[0]
    emb_grad = (x_grad + grad_part.astype(jnp.float32)).astype(jnp.bfloat16)
    return (emb_grad, w_in_term, w_out_term)

def row_adam(rows_now, mom_now, var_now, grad, counts):
    touched = counts > 0.5
    mom_next = beta_one * mom_now + (1.0 - beta_one) * grad
    var_next = beta_two * var_now + (1.0 - beta_two) * lax.optimization_barrier(jnp.mean(grad * grad, axis=1))
    advance = mom_next / bias_one / (jnp.sqrt(var_next / bias_two)[:, None] + adam_eps)
    rows_next = rows_now - learn_rate * advance
    return (jnp.where(touched[:, None], rows_next, rows_now), jnp.where(touched[:, None], mom_next, mom_now), jnp.where(touched, var_next, var_now))

def reference(tokens, out_grad, seq_lengths, owners, slots, w_in, w_out, emb_rows, emb_mom, emb_var):
    x_blocks = tokens.reshape(DEVICES, TOK_DEV, D)
    g_blocks = out_grad.reshape(DEVICES, TOK_DEV, D)

    def advance_block(totals, inputs_now):
        x_part, grad_part, lengths = inputs_now
        emb_grad, w_in_term, w_out_term = device_grads(x_part, grad_part, lengths, w_in, w_out)
        return ((totals[0] + w_in_term, totals[1] + w_out_term), emb_grad)
    start = (jnp.zeros((D, 4 * HW), jnp.float32), jnp.zeros((D, HW), jnp.float32))
    (w_in_grad, w_out_grad), emb_blocks = lax.scan(advance_block, start, (x_blocks, g_blocks, seq_lengths))
    emb_grad = emb_blocks.reshape(TOKENS, D)
    row_index = (owners[:, 0] * SLOTS + slots).astype(jnp.int32)
    row_grad = jax.ops.segment_sum(emb_grad.astype(jnp.float32), row_index, num_segments=TABLE)
    row_count = jax.ops.segment_sum(jnp.ones((TOKENS,), jnp.float32), row_index, num_segments=TABLE)
    new_rows, new_mom, new_var = row_adam(emb_rows, emb_mom, emb_var, row_grad, row_count)
    return (new_rows, new_mom, new_var, w_in_grad, w_out_grad)
```

```python
import functools

import jax
import jax.numpy as jnp
from jax import lax
from jax.sharding import Mesh, PartitionSpec as P

HEADS = 4
HEAD_DIM = 64
HW = 256
MAXLEN = 256


norm_eps = 1e-06
beta_one = 0.9
beta_two = 0.99
learn_rate = 0.05
adam_eps = 1e-08
bias_one = 1.0 - 0.9**10
bias_two = 1.0 - 0.99**10


def layer_norm(values):
    average = jnp.mean(values, axis=-1, keepdims=True)
    centered = values - average
    spread = jnp.mean(centered * centered, axis=-1, keepdims=True)
    return centered * lax.rsqrt(spread + norm_eps)


def allowed_mask(lengths, tok_count):
    ends = jnp.cumsum(lengths)
    position = jnp.arange(tok_count, dtype=jnp.int32)
    segment = jnp.sum((position[:, None] >= ends[None, :]).astype(jnp.int32), axis=1)
    same = segment[:, None] == segment[None, :]
    causal = position[None, :] <= position[:, None]
    return (same & causal).astype(jnp.float32)


def core(pre, allowed):
    tok_count = pre.shape[0]
    proj = jax.nn.silu(pre).astype(jnp.bfloat16)
    upart, vpart, qpart, kpart = jnp.split(proj, 4, axis=1)
    queries = qpart.reshape(tok_count, HEADS, HEAD_DIM)
    keys_part = kpart.reshape(tok_count, HEADS, HEAD_DIM)
    values_part = vpart.reshape(tok_count, HEADS, HEAD_DIM)
    scores = jnp.einsum(
        "thd,shd->hts", queries, keys_part, preferred_element_type=jnp.float32
    ) * HEAD_DIM ** (-0.5)
    weights = (jax.nn.silu(scores) * allowed[None] / MAXLEN).astype(jnp.bfloat16)
    attn = jnp.einsum(
        "hts,shd->thd", weights, values_part, preferred_element_type=jnp.float32
    ).reshape(tok_count, HW)
    return (layer_norm(attn) * upart.astype(jnp.float32)).astype(jnp.bfloat16)


def row_adam(rows_now, mom_now, var_now, grad, counts):
    touched = counts > 0.5
    mom_next = beta_one * mom_now + (1.0 - beta_one) * grad
    var_next = beta_two * var_now + (1.0 - beta_two) * jnp.mean(grad * grad, axis=1)
    advance = mom_next / bias_one / (jnp.sqrt(var_next / bias_two)[:, None] + adam_eps)
    rows_next = rows_now - learn_rate * advance
    return (
        jnp.where(touched[:, None], rows_next, rows_now),
        jnp.where(touched[:, None], mom_next, mom_now),
        jnp.where(touched, var_next, var_now),
    )


ROW_AXES = ("z", "y", "core")
ALL_AXES = ("z", "y", "core", "x")


def reduce_weights(partial, sizes):
    width = partial.shape[1]
    blocks = partial.reshape(tuple(sizes[a] for a in ROW_AXES) + (-1, width))
    for i, ax in enumerate(ROW_AXES):
        moved = jnp.moveaxis(blocks, i, 0)
        rest = moved.shape[1:]
        flat = moved.reshape(moved.shape[0], -1, 128)
        flat = lax.psum_scatter(flat, ax, scatter_dimension=0, tiled=True)
        blocks = jnp.moveaxis(flat.reshape((1,) + rest), 0, i)
    return lax.psum(blocks.reshape(-1, width), "x")


def local(sizes, tokens, out_grad, seq_lengths, owners, slots, w_in, w_out, emb_rows, emb_mom, emb_var):
    tok_count = tokens.shape[0]
    width = tokens.shape[1]
    allowed = allowed_mask(seq_lengths[0], tok_count)
    normed_exact, norm_back = jax.vjp(layer_norm, tokens.astype(jnp.float32))
    normed = normed_exact.astype(jnp.bfloat16)
    pre = jnp.dot(normed, w_in, preferred_element_type=jnp.float32)
    y_out, core_back = jax.vjp(lambda inner: core(inner, allowed), pre)
    y_grad = jnp.dot(out_grad, w_out, preferred_element_type=jnp.float32).astype(jnp.bfloat16)
    pre_grad_b = core_back(y_grad)[0].astype(jnp.bfloat16)
    normed_grad = lax.dot_general(
        pre_grad_b, w_in, (((1,), (1,)), ((), ())), preferred_element_type=jnp.float32
    )
    emb_grad = (norm_back(normed_grad)[0] + out_grad.astype(jnp.float32)).astype(jnp.bfloat16)
    contract = (((0,), (0,)), ((), ()))
    in_cols = w_in.shape[1]
    owner_count = 1
    for a in ROW_AXES:
        owner_count *= sizes[a]
    weight_share = reduce_weights(
        jnp.concatenate(
            [
                lax.dot_general(normed, pre_grad_b, contract, preferred_element_type=jnp.float32),
                lax.dot_general(out_grad, y_out, contract, preferred_element_type=jnp.float32),
            ],
            axis=1,
        ),
        sizes,
    )
    w_in_grad = weight_share[:, :in_cols]
    w_out_grad = weight_share[:, in_cols:]
    capacity = max(2, 4 * tok_count // owner_count)
    buffer_rows = owner_count * capacity
    owner_of = owners[:, 0]
    position = jnp.arange(tok_count, dtype=jnp.int32)
    earlier = jnp.sum(
        ((owner_of[:, None] == owner_of[None, :]) & (position[None, :] < position[:, None])).astype(
            jnp.int32
        ),
        axis=1,
    )
    position_to = owner_of * capacity + earlier
    chosen = position_to[None, :] == jnp.arange(buffer_rows, dtype=jnp.int32)[:, None]
    outgoing = jnp.dot(
        chosen.astype(jnp.bfloat16), emb_grad, preferred_element_type=jnp.float32
    ).astype(jnp.bfloat16)
    outgoing = outgoing.reshape(owner_count, capacity, width)
    out_slots = (jnp.sum(jnp.where(chosen, slots[None, :] + 1, 0), axis=1) - 1).reshape(
        owner_count, capacity
    )
    slot_row = jnp.zeros((owner_count, 1, width), jnp.bfloat16)
    slot_row = slot_row.at[:, 0, :capacity].set(out_slots.astype(jnp.bfloat16))
    arrived = lax.all_to_all(
        jnp.concatenate([outgoing, slot_row], axis=1), ROW_AXES, 0, 0, tiled=True
    )
    received = arrived[:, :capacity, :].reshape(buffer_rows, width)
    got_slots = arrived[:, capacity, :capacity].astype(jnp.int32).reshape(buffer_rows)
    slot_count = emb_rows.shape[0]
    matches = got_slots[None, :] == jnp.arange(slot_count, dtype=jnp.int32)[:, None]
    grad_part = jnp.dot(matches.astype(jnp.bfloat16), received, preferred_element_type=jnp.float32)
    count_part = jnp.sum(matches.astype(jnp.float32), axis=1)
    grad_all, count_all = lax.psum((grad_part, count_part), "x")
    new_rows, new_mom, new_var = row_adam(emb_rows, emb_mom, emb_var, grad_all, count_all)
    return (new_rows, new_mom, new_var, w_in_grad, w_out_grad)


def solution(mesh):
    n_rows, n_dp = mesh.shape["rows"], mesh.shape["dp"]
    sizes = {"core": 2, "y": 4}
    sizes["z"] = n_rows // (sizes["core"] * sizes["y"])
    sizes["x"] = n_dp
    fine = Mesh(
        mesh.devices.reshape(sizes["z"], sizes["y"], sizes["core"], sizes["x"]), ALL_AXES
    )
    tok = P(ALL_AXES, None)
    own = P(ROW_AXES, None)
    in_specs = (tok, tok, tok, tok, P(ALL_AXES), P(), P(), own, own, P(ROW_AXES))
    out_specs = (own, own, P(ROW_AXES), own, own)
    return jax.shard_map(
        functools.partial(local, sizes), mesh=fine, in_specs=in_specs, out_specs=out_specs,
        check_vma=False,
    )
```

```python
import functools

import jax
import jax.numpy as jnp
from jax import lax
from jax.sharding import Mesh, PartitionSpec as P

HEADS = 4
HEAD_DIM = 64
HW = 256
MAXLEN = 256


norm_eps = 1e-06
beta_one = 0.9
beta_two = 0.99
learn_rate = 0.05
adam_eps = 1e-08
bias_one = 1.0 - 0.9**10
bias_two = 1.0 - 0.99**10


def layer_norm(values):
    average = jnp.mean(values, axis=-1, keepdims=True)
    centered = values - average
    spread = jnp.mean(centered * centered, axis=-1, keepdims=True)
    return centered * lax.rsqrt(spread + norm_eps)


def allowed_mask(lengths, tok_count):
    ends = jnp.cumsum(lengths)
    position = jnp.arange(tok_count, dtype=jnp.int32)
    segment = jnp.sum((position[:, None] >= ends[None, :]).astype(jnp.int32), axis=1)
    same = segment[:, None] == segment[None, :]
    causal = position[None, :] <= position[:, None]
    return (same & causal).astype(jnp.float32)


def core(pre, allowed):
    tok_count = pre.shape[0]
    proj = jax.nn.silu(pre).astype(jnp.bfloat16)
    upart, vpart, qpart, kpart = jnp.split(proj, 4, axis=1)
    queries = qpart.reshape(tok_count, HEADS, HEAD_DIM)
    keys_part = kpart.reshape(tok_count, HEADS, HEAD_DIM)
    values_part = vpart.reshape(tok_count, HEADS, HEAD_DIM)
    scores = jnp.einsum(
        "thd,shd->hts", queries, keys_part, preferred_element_type=jnp.float32
    ) * HEAD_DIM ** (-0.5)
    weights = (jax.nn.silu(scores) * allowed[None] / MAXLEN).astype(jnp.bfloat16)
    attn = jnp.einsum(
        "hts,shd->thd", weights, values_part, preferred_element_type=jnp.float32
    ).reshape(tok_count, HW)
    return (layer_norm(attn) * upart.astype(jnp.float32)).astype(jnp.bfloat16)


def row_adam(rows_now, mom_now, var_now, grad, counts):
    touched = counts > 0.5
    mom_next = beta_one * mom_now + (1.0 - beta_one) * grad
    var_next = beta_two * var_now + (1.0 - beta_two) * jnp.mean(grad * grad, axis=1)
    advance = mom_next / bias_one / (jnp.sqrt(var_next / bias_two)[:, None] + adam_eps)
    rows_next = rows_now - learn_rate * advance
    return (
        jnp.where(touched[:, None], rows_next, rows_now),
        jnp.where(touched[:, None], mom_next, mom_now),
        jnp.where(touched, var_next, var_now),
    )


ROW_AXES = ("z", "y", "core")
ALL_AXES = ("z", "y", "core", "x")


def shifted(value, axis, size, step):
    return lax.ppermute(value, axis, [(i, (i + step) % size) for i in range(size)])


def scatter_sum(blocks, axis, size, dim):
    me = lax.axis_index(axis)
    total = lax.dynamic_index_in_dim(blocks, me, dim, keepdims=False)
    for step in range(1, size):
        piece = lax.dynamic_index_in_dim(blocks, (me + step) % size, dim, keepdims=False)
        total = total + shifted(piece, axis, size, step)
    return total


def gather_rows(row, axis, size):
    me = lax.axis_index(axis)
    pieces = [row]
    for step in range(1, size):
        pieces.append(shifted(row, axis, size, step))
    stacked = jnp.stack(pieces)
    order = (me - jnp.arange(size)) % size
    return jnp.zeros_like(stacked).at[order].set(stacked)


def reduce_weights(partial, sizes):
    width = partial.shape[1]
    per_owner = partial.shape[0] // (sizes["z"] * sizes["y"] * sizes["core"])
    blocks = partial.reshape(sizes["z"], sizes["y"], sizes["core"], per_owner, width)
    blocks = scatter_sum(blocks, "core", sizes["core"], 2)
    blocks = blocks.reshape(sizes["z"], sizes["y"], sizes["x"], per_owner // sizes["x"], width)
    blocks = scatter_sum(blocks, "x", sizes["x"], 2)
    blocks = scatter_sum(blocks, "y", sizes["y"], 1)
    blocks = scatter_sum(blocks, "z", sizes["z"], 0)
    return gather_rows(blocks, "x", sizes["x"]).reshape(per_owner, width)


def sum_over(value, axis, size):
    total = value
    for step in range(1, size):
        total = total + shifted(value, axis, size, step)
    return total


def local(sizes, tokens, out_grad, seq_lengths, owners, slots, w_in, w_out, emb_rows, emb_mom, emb_var):
    tok_count = tokens.shape[0]
    width = tokens.shape[1]
    allowed = allowed_mask(seq_lengths[0], tok_count)
    normed_exact, norm_back = jax.vjp(layer_norm, tokens.astype(jnp.float32))
    normed = normed_exact.astype(jnp.bfloat16)
    pre = jnp.dot(normed, w_in, preferred_element_type=jnp.float32)
    y_out, core_back = jax.vjp(lambda inner: core(inner, allowed), pre)
    y_grad = jnp.dot(out_grad, w_out, preferred_element_type=jnp.float32).astype(jnp.bfloat16)
    pre_grad_b = core_back(y_grad)[0].astype(jnp.bfloat16)
    normed_grad = lax.dot_general(
        pre_grad_b, w_in, (((1,), (1,)), ((), ())), preferred_element_type=jnp.float32
    )
    emb_grad = (norm_back(normed_grad)[0] + out_grad.astype(jnp.float32)).astype(jnp.bfloat16)
    contract = (((0,), (0,)), ((), ()))
    in_cols = w_in.shape[1]
    owner_count = 1
    for a in ROW_AXES:
        owner_count *= sizes[a]
    weight_share = reduce_weights(
        jnp.concatenate(
            [
                lax.dot_general(normed, pre_grad_b, contract, preferred_element_type=jnp.float32),
                lax.dot_general(out_grad, y_out, contract, preferred_element_type=jnp.float32),
            ],
            axis=1,
        ),
        sizes,
    )
    w_in_grad = weight_share[:, :in_cols]
    w_out_grad = weight_share[:, in_cols:]
    capacity = max(2, 4 * tok_count // owner_count)
    buffer_rows = owner_count * capacity
    owner_of = owners[:, 0]
    position = jnp.arange(tok_count, dtype=jnp.int32)
    earlier = jnp.sum(
        ((owner_of[:, None] == owner_of[None, :]) & (position[None, :] < position[:, None])).astype(
            jnp.int32
        ),
        axis=1,
    )
    position_to = owner_of * capacity + earlier
    chosen = position_to[None, :] == jnp.arange(buffer_rows, dtype=jnp.int32)[:, None]
    outgoing = jnp.dot(
        chosen.astype(jnp.bfloat16), emb_grad, preferred_element_type=jnp.float32
    ).astype(jnp.bfloat16)
    outgoing = outgoing.reshape(owner_count, capacity, width)
    out_slots = (jnp.sum(jnp.where(chosen, slots[None, :] + 1, 0), axis=1) - 1).reshape(
        owner_count, capacity
    )
    slot_row = jnp.zeros((owner_count, 1, width), jnp.bfloat16)
    slot_row = slot_row.at[:, 0, :capacity].set(out_slots.astype(jnp.bfloat16))
    arrived = lax.all_to_all(
        jnp.concatenate([outgoing, slot_row], axis=1), ROW_AXES, 0, 0, tiled=True
    )
    received = arrived[:, :capacity, :].reshape(buffer_rows, width)
    got_slots = arrived[:, capacity, :capacity].astype(jnp.int32).reshape(buffer_rows)
    slot_count = emb_rows.shape[0]
    matches = got_slots[None, :] == jnp.arange(slot_count, dtype=jnp.int32)[:, None]
    grad_part = jnp.dot(matches.astype(jnp.bfloat16), received, preferred_element_type=jnp.float32)
    count_part = jnp.sum(matches.astype(jnp.float32), axis=1)
    both = sum_over(
        jnp.concatenate([grad_part, jnp.broadcast_to(count_part[:, None], (slot_count, 128))], axis=1),
        "x",
        sizes["x"],
    )
    grad_all, count_all = both[:, :width], both[:, width]
    new_rows, new_mom, new_var = row_adam(emb_rows, emb_mom, emb_var, grad_all, count_all)
    return (new_rows, new_mom, new_var, w_in_grad, w_out_grad)


def solution(mesh):
    n_rows, n_dp = mesh.shape["rows"], mesh.shape["dp"]
    sizes = {"core": 2, "y": 4}
    sizes["z"] = n_rows // (sizes["core"] * sizes["y"])
    sizes["x"] = n_dp
    fine = Mesh(
        mesh.devices.reshape(sizes["z"], sizes["y"], sizes["core"], sizes["x"]), ALL_AXES
    )
    tok = P(ALL_AXES, None)
    own = P(ROW_AXES, None)
    in_specs = (tok, tok, tok, tok, P(ALL_AXES), P(), P(), own, own, P(ROW_AXES))
    out_specs = (own, own, P(ROW_AXES), own, own)
    return jax.shard_map(
        functools.partial(local, sizes), mesh=fine, in_specs=in_specs, out_specs=out_specs,
        check_vma=False,
    )
```

```python
import functools

import jax
import jax.numpy as jnp
from jax import lax
from jax.sharding import Mesh, PartitionSpec as P

HEADS = 4
HEAD_DIM = 64
HW = 256
MAXLEN = 256


norm_eps = 1e-06
beta_one = 0.9
beta_two = 0.99
learn_rate = 0.05
adam_eps = 1e-08
bias_one = 1.0 - 0.9**10
bias_two = 1.0 - 0.99**10


def layer_norm(values):
    average = jnp.mean(values, axis=-1, keepdims=True)
    centered = values - average
    spread = jnp.mean(centered * centered, axis=-1, keepdims=True)
    return centered * lax.rsqrt(spread + norm_eps)


def allowed_mask(lengths, tok_count):
    ends = jnp.cumsum(lengths)
    position = jnp.arange(tok_count, dtype=jnp.int32)
    segment = jnp.sum((position[:, None] >= ends[None, :]).astype(jnp.int32), axis=1)
    same = segment[:, None] == segment[None, :]
    causal = position[None, :] <= position[:, None]
    return (same & causal).astype(jnp.float32)


def core(pre, allowed):
    tok_count = pre.shape[0]
    proj = jax.nn.silu(pre).astype(jnp.bfloat16)
    upart, vpart, qpart, kpart = jnp.split(proj, 4, axis=1)
    queries = qpart.reshape(tok_count, HEADS, HEAD_DIM)
    keys_part = kpart.reshape(tok_count, HEADS, HEAD_DIM)
    values_part = vpart.reshape(tok_count, HEADS, HEAD_DIM)
    scores = jnp.einsum(
        "thd,shd->hts", queries, keys_part, preferred_element_type=jnp.float32
    ) * HEAD_DIM ** (-0.5)
    weights = (jax.nn.silu(scores) * allowed[None] / MAXLEN).astype(jnp.bfloat16)
    attn = jnp.einsum(
        "hts,shd->thd", weights, values_part, preferred_element_type=jnp.float32
    ).reshape(tok_count, HW)
    return (layer_norm(attn) * upart.astype(jnp.float32)).astype(jnp.bfloat16)


def row_adam(rows_now, mom_now, var_now, grad, counts):
    touched = counts > 0.5
    mom_next = beta_one * mom_now + (1.0 - beta_one) * grad
    var_next = beta_two * var_now + (1.0 - beta_two) * jnp.mean(grad * grad, axis=1)
    advance = mom_next / bias_one / (jnp.sqrt(var_next / bias_two)[:, None] + adam_eps)
    rows_next = rows_now - learn_rate * advance
    return (
        jnp.where(touched[:, None], rows_next, rows_now),
        jnp.where(touched[:, None], mom_next, mom_now),
        jnp.where(touched, var_next, var_now),
    )


ROW_AXES = ("z", "y", "core")
ALL_AXES = ("z", "y", "core", "x")


def moved(value, axis, pairs):
    return lax.ppermute(value, axis, pairs)


def scatter_sum(blocks, axis, me, pairs_of, size, dim):
    total = lax.dynamic_index_in_dim(blocks, me, dim, keepdims=False)
    for step in range(1, size):
        piece = lax.dynamic_index_in_dim(blocks, (me + step) % size, dim, keepdims=False)
        total = total + moved(piece, axis, pairs_of(step))
    return total


def ring(total, size, group=1):
    span = size * group

    def pairs_of(step):
        return [
            (i, (i // span) * span + (i % group) + ((i % span) // group + step) % size * group)
            for i in range(total)
        ]

    return pairs_of


def reduce_weights(partial, sizes):
    width = partial.shape[1]
    n_z, n_y, n_c, n_x = sizes["z"], sizes["y"], sizes["core"], sizes["x"]
    per_owner = partial.shape[0] // (n_z * n_y * n_c)
    blocks = partial.reshape(n_z, n_y, n_c, per_owner, width)
    blocks = scatter_sum(blocks, "core", lax.axis_index("core"), ring(n_c, n_c), n_c, 2)
    blocks = scatter_sum(blocks, "y", lax.axis_index("y"), ring(n_y, n_y), n_y, 1)
    z_lo = 4 if n_z % 4 == 0 else 1
    z_hi = n_z // z_lo
    z_me = lax.axis_index("z")
    blocks = blocks.reshape(z_hi, z_lo, per_owner, width)
    blocks = scatter_sum(blocks, "z", z_me % z_lo, ring(n_z, z_lo), z_lo, 1)
    blocks = scatter_sum(blocks, "z", z_me // z_lo, ring(n_z, z_hi, z_lo), z_hi, 0)
    return sum_over(blocks, "x", n_x)


def sum_over(value, axis, size):
    total = value
    for step in range(1, size):
        total = total + moved(value, axis, ring(size, size)(step))
    return total


def local(sizes, tokens, out_grad, seq_lengths, owners, slots, w_in, w_out, emb_rows, emb_mom, emb_var):
    tok_count = tokens.shape[0]
    width = tokens.shape[1]
    allowed = allowed_mask(seq_lengths[0], tok_count)
    normed_exact, norm_back = jax.vjp(layer_norm, tokens.astype(jnp.float32))
    normed = normed_exact.astype(jnp.bfloat16)
    pre = jnp.dot(normed, w_in, preferred_element_type=jnp.float32)
    y_out, core_back = jax.vjp(lambda inner: core(inner, allowed), pre)
    y_grad = jnp.dot(out_grad, w_out, preferred_element_type=jnp.float32).astype(jnp.bfloat16)
    pre_grad_b = core_back(y_grad)[0].astype(jnp.bfloat16)
    normed_grad = lax.dot_general(
        pre_grad_b, w_in, (((1,), (1,)), ((), ())), preferred_element_type=jnp.float32
    )
    emb_grad = (norm_back(normed_grad)[0] + out_grad.astype(jnp.float32)).astype(jnp.bfloat16)
    contract = (((0,), (0,)), ((), ()))
    in_cols = w_in.shape[1]
    owner_count = 1
    for a in ROW_AXES:
        owner_count *= sizes[a]
    weight_share = reduce_weights(
        jnp.concatenate(
            [
                lax.dot_general(normed, pre_grad_b, contract, preferred_element_type=jnp.float32),
                lax.dot_general(out_grad, y_out, contract, preferred_element_type=jnp.float32),
            ],
            axis=1,
        ),
        sizes,
    )
    capacity = max(2, 4 * tok_count // owner_count)
    buffer_rows = owner_count * capacity
    owner_of = owners[:, 0]
    position = jnp.arange(tok_count, dtype=jnp.int32)
    earlier = jnp.sum(
        ((owner_of[:, None] == owner_of[None, :]) & (position[None, :] < position[:, None])).astype(
            jnp.int32
        ),
        axis=1,
    )
    position_to = owner_of * capacity + earlier
    chosen = position_to[None, :] == jnp.arange(buffer_rows, dtype=jnp.int32)[:, None]
    outgoing = jnp.dot(
        chosen.astype(jnp.bfloat16), emb_grad, preferred_element_type=jnp.float32
    ).astype(jnp.bfloat16)
    outgoing = outgoing.reshape(owner_count, capacity, width)
    out_slots = (jnp.sum(jnp.where(chosen, slots[None, :] + 1, 0), axis=1) - 1).reshape(
        owner_count, capacity
    )
    slot_row = jnp.zeros((owner_count, 1, width), jnp.bfloat16)
    slot_row = slot_row.at[:, 0, :capacity].set(out_slots.astype(jnp.bfloat16))
    arrived = lax.all_to_all(
        jnp.concatenate([outgoing, slot_row], axis=1), ROW_AXES, 0, 0, tiled=True
    )
    arrived, weight_share = lax.optimization_barrier((arrived, weight_share))
    w_in_grad = weight_share[:, :in_cols]
    w_out_grad = weight_share[:, in_cols:]
    received = arrived[:, :capacity, :].reshape(buffer_rows, width)
    got_slots = arrived[:, capacity, :capacity].astype(jnp.int32).reshape(buffer_rows)
    slot_count = emb_rows.shape[0]
    matches = got_slots[None, :] == jnp.arange(slot_count, dtype=jnp.int32)[:, None]
    grad_part = jnp.dot(matches.astype(jnp.bfloat16), received, preferred_element_type=jnp.float32)
    count_part = jnp.sum(matches.astype(jnp.float32), axis=1)
    both = sum_over(
        jnp.concatenate([grad_part, jnp.broadcast_to(count_part[:, None], (slot_count, 128))], axis=1),
        "x",
        sizes["x"],
    )
    grad_all, count_all = both[:, :width], both[:, width]
    new_rows, new_mom, new_var = row_adam(emb_rows, emb_mom, emb_var, grad_all, count_all)
    return (new_rows, new_mom, new_var, w_in_grad, w_out_grad)


def solution(mesh):
    n_rows, n_dp = mesh.shape["rows"], mesh.shape["dp"]
    sizes = {"core": 2, "y": 4}
    sizes["z"] = n_rows // (sizes["core"] * sizes["y"])
    sizes["x"] = n_dp
    fine = Mesh(
        mesh.devices.reshape(sizes["z"], sizes["y"], sizes["core"], sizes["x"]), ALL_AXES
    )
    tok = P(ALL_AXES, None)
    own = P(ROW_AXES, None)
    in_specs = (tok, tok, tok, tok, P(ALL_AXES), P(), P(), own, own, P(ROW_AXES))
    out_specs = (own, own, P(ROW_AXES), own, own)
    return jax.shard_map(
        functools.partial(local, sizes), mesh=fine, in_specs=in_specs, out_specs=out_specs,
        check_vma=False,
    )
```

```python
import functools

import jax
import jax.numpy as jnp
from jax import lax
from jax.sharding import Mesh, PartitionSpec as P

HEADS = 4
HEAD_DIM = 64
HW = 256
MAXLEN = 256


norm_eps = 1e-06
beta_one = 0.9
beta_two = 0.99
learn_rate = 0.05
adam_eps = 1e-08
bias_one = 1.0 - 0.9**10
bias_two = 1.0 - 0.99**10


def layer_norm(values):
    average = jnp.mean(values, axis=-1, keepdims=True)
    centered = values - average
    spread = jnp.mean(centered * centered, axis=-1, keepdims=True)
    return centered * lax.rsqrt(spread + norm_eps)


def allowed_mask(lengths, tok_count):
    ends = jnp.cumsum(lengths)
    position = jnp.arange(tok_count, dtype=jnp.int32)
    segment = jnp.sum((position[:, None] >= ends[None, :]).astype(jnp.int32), axis=1)
    same = segment[:, None] == segment[None, :]
    causal = position[None, :] <= position[:, None]
    return (same & causal).astype(jnp.float32)


def core(pre, allowed):
    tok_count = pre.shape[0]
    proj = jax.nn.silu(pre).astype(jnp.bfloat16)
    upart, vpart, qpart, kpart = jnp.split(proj, 4, axis=1)
    queries = qpart.reshape(tok_count, HEADS, HEAD_DIM)
    keys_part = kpart.reshape(tok_count, HEADS, HEAD_DIM)
    values_part = vpart.reshape(tok_count, HEADS, HEAD_DIM)
    scores = jnp.einsum(
        "thd,shd->hts", queries, keys_part, preferred_element_type=jnp.float32
    ) * HEAD_DIM ** (-0.5)
    weights = (jax.nn.silu(scores) * allowed[None] / MAXLEN).astype(jnp.bfloat16)
    attn = jnp.einsum(
        "hts,shd->thd", weights, values_part, preferred_element_type=jnp.float32
    ).reshape(tok_count, HW)
    return (layer_norm(attn) * upart.astype(jnp.float32)).astype(jnp.bfloat16)


def row_adam(rows_now, mom_now, var_now, grad, counts):
    touched = counts > 0.5
    mom_next = beta_one * mom_now + (1.0 - beta_one) * grad
    var_next = beta_two * var_now + (1.0 - beta_two) * jnp.mean(grad * grad, axis=1)
    advance = mom_next / bias_one / (jnp.sqrt(var_next / bias_two)[:, None] + adam_eps)
    rows_next = rows_now - learn_rate * advance
    return (
        jnp.where(touched[:, None], rows_next, rows_now),
        jnp.where(touched[:, None], mom_next, mom_now),
        jnp.where(touched, var_next, var_now),
    )


ROW_AXES = ("z", "y", "core")
ALL_AXES = ("z", "y", "core", "x")


def halve_sum(blocks, axis, size, dim):
    me = lax.axis_index(axis)
    lead = blocks.shape[:dim]
    bits = size.bit_length() - 1
    blocks = blocks.reshape(lead + (2,) * bits + blocks.shape[dim + 1 :])
    for bit in range(bits):
        at = dim + bits - 1 - bit
        mine = (me >> bit) & 1
        keep = lax.dynamic_index_in_dim(blocks, mine, at, keepdims=True)
        send = lax.dynamic_index_in_dim(blocks, 1 - mine, at, keepdims=True)
        pairs = [(i, i ^ (1 << bit)) for i in range(size)]
        blocks = keep + lax.ppermute(send, axis, pairs)
    return blocks.reshape(lead + blocks.shape[dim + bits :])


def double_sum(value, axis, size):
    for bit in range(size.bit_length() - 1):
        value = value + lax.ppermute(value, axis, [(i, i ^ (1 << bit)) for i in range(size)])
    return value


def reduce_weights(partial, sizes):
    width = partial.shape[1]
    n_z, n_y, n_c = sizes["z"], sizes["y"], sizes["core"]
    per_owner = partial.shape[0] // (n_z * n_y * n_c)
    blocks = partial.reshape(n_z, n_y, n_c, per_owner, width)
    blocks = halve_sum(blocks, "core", n_c, 2)
    blocks = halve_sum(blocks, "y", n_y, 1)
    blocks = halve_sum(blocks, "z", n_z, 0)
    return blocks.reshape(per_owner, width)


def local(sizes, tokens, out_grad, seq_lengths, owners, slots, w_in, w_out, emb_rows, emb_mom, emb_var):
    tok_count = tokens.shape[0]
    width = tokens.shape[1]
    allowed = allowed_mask(seq_lengths[0], tok_count)
    normed_exact, norm_back = jax.vjp(layer_norm, tokens.astype(jnp.float32))
    normed = normed_exact.astype(jnp.bfloat16)
    pre = jnp.dot(normed, w_in, preferred_element_type=jnp.float32)
    y_out, core_back = jax.vjp(lambda inner: core(inner, allowed), pre)
    y_grad = jnp.dot(out_grad, w_out, preferred_element_type=jnp.float32).astype(jnp.bfloat16)
    pre_grad_b = core_back(y_grad)[0].astype(jnp.bfloat16)
    normed_grad = lax.dot_general(
        pre_grad_b, w_in, (((1,), (1,)), ((), ())), preferred_element_type=jnp.float32
    )
    emb_grad = (norm_back(normed_grad)[0] + out_grad.astype(jnp.float32)).astype(jnp.bfloat16)
    contract = (((0,), (0,)), ((), ()))
    in_cols = w_in.shape[1]
    owner_count = 1
    for a in ROW_AXES:
        owner_count *= sizes[a]
    weight_share = reduce_weights(
        jnp.concatenate(
            [
                lax.dot_general(normed, pre_grad_b, contract, preferred_element_type=jnp.float32),
                lax.dot_general(out_grad, y_out, contract, preferred_element_type=jnp.float32),
            ],
            axis=1,
        ),
        sizes,
    )
    capacity = max(2, 4 * tok_count // owner_count)
    buffer_rows = owner_count * capacity
    owner_of = owners[:, 0]
    position = jnp.arange(tok_count, dtype=jnp.int32)
    earlier = jnp.sum(
        ((owner_of[:, None] == owner_of[None, :]) & (position[None, :] < position[:, None])).astype(
            jnp.int32
        ),
        axis=1,
    )
    position_to = owner_of * capacity + earlier
    chosen = position_to[None, :] == jnp.arange(buffer_rows, dtype=jnp.int32)[:, None]
    outgoing = jnp.dot(
        chosen.astype(jnp.bfloat16), emb_grad, preferred_element_type=jnp.float32
    ).astype(jnp.bfloat16)
    outgoing = outgoing.reshape(owner_count, capacity, width)
    out_slots = (jnp.sum(jnp.where(chosen, slots[None, :] + 1, 0), axis=1) - 1).reshape(
        owner_count, capacity
    )
    slot_row = jnp.zeros((owner_count, 1, width), jnp.bfloat16)
    slot_row = slot_row.at[:, 0, :capacity].set(out_slots.astype(jnp.bfloat16))
    arrived = lax.all_to_all(
        jnp.concatenate([outgoing, slot_row], axis=1), ROW_AXES, 0, 0, tiled=True
    )
    arrived, weight_share = lax.optimization_barrier((arrived, weight_share))
    received = arrived[:, :capacity, :].reshape(buffer_rows, width)
    got_slots = arrived[:, capacity, :capacity].astype(jnp.int32).reshape(buffer_rows)
    slot_count = emb_rows.shape[0]
    matches = got_slots[None, :] == jnp.arange(slot_count, dtype=jnp.int32)[:, None]
    grad_part = jnp.dot(matches.astype(jnp.bfloat16), received, preferred_element_type=jnp.float32)
    count_part = jnp.sum(matches.astype(jnp.float32), axis=1)
    lanes = width + 128
    both = double_sum(
        jnp.concatenate(
            [
                jnp.concatenate(
                    [grad_part, jnp.broadcast_to(count_part[:, None], (slot_count, 128))], axis=1
                ),
                weight_share.reshape(-1, lanes),
            ],
            axis=0,
        ),
        "x",
        sizes["x"],
    )
    grad_all, count_all = both[:slot_count, :width], both[:slot_count, width]
    weight_share = both[slot_count:].reshape(weight_share.shape)
    w_in_grad = weight_share[:, :in_cols]
    w_out_grad = weight_share[:, in_cols:]
    new_rows, new_mom, new_var = row_adam(emb_rows, emb_mom, emb_var, grad_all, count_all)
    return (new_rows, new_mom, new_var, w_in_grad, w_out_grad)


def solution(mesh):
    n_rows, n_dp = mesh.shape["rows"], mesh.shape["dp"]
    sizes = {"core": 2, "y": 4}
    sizes["z"] = n_rows // (sizes["core"] * sizes["y"])
    sizes["x"] = n_dp
    fine = Mesh(
        mesh.devices.reshape(sizes["z"], sizes["y"], sizes["core"], sizes["x"]), ALL_AXES
    )
    tok = P(ALL_AXES, None)
    own = P(ROW_AXES, None)
    in_specs = (tok, tok, tok, tok, P(ALL_AXES), P(), P(), own, own, P(ROW_AXES))
    out_specs = (own, own, P(ROW_AXES), own, own)
    return jax.shard_map(
        functools.partial(local, sizes), mesh=fine, in_specs=in_specs, out_specs=out_specs,
        check_vma=False,
    )
```

```python
import functools

import jax
import jax.numpy as jnp
from jax import lax
from jax.sharding import Mesh, PartitionSpec as P

HEADS = 4
HEAD_DIM = 64
HW = 256
MAXLEN = 256


norm_eps = 1e-06
beta_one = 0.9
beta_two = 0.99
learn_rate = 0.05
adam_eps = 1e-08
bias_one = 1.0 - 0.9**10
bias_two = 1.0 - 0.99**10


def layer_norm(values):
    average = jnp.mean(values, axis=-1, keepdims=True)
    centered = values - average
    spread = jnp.mean(centered * centered, axis=-1, keepdims=True)
    return centered * lax.rsqrt(spread + norm_eps)


def allowed_mask(lengths, tok_count):
    ends = jnp.cumsum(lengths)
    position = jnp.arange(tok_count, dtype=jnp.int32)
    segment = jnp.sum((position[:, None] >= ends[None, :]).astype(jnp.int32), axis=1)
    same = segment[:, None] == segment[None, :]
    causal = position[None, :] <= position[:, None]
    return (same & causal).astype(jnp.float32)


def core(pre, allowed):
    tok_count = pre.shape[0]
    proj = jax.nn.silu(pre).astype(jnp.bfloat16)
    upart, vpart, qpart, kpart = jnp.split(proj, 4, axis=1)
    queries = qpart.reshape(tok_count, HEADS, HEAD_DIM)
    keys_part = kpart.reshape(tok_count, HEADS, HEAD_DIM)
    values_part = vpart.reshape(tok_count, HEADS, HEAD_DIM)
    scores = jnp.einsum(
        "thd,shd->hts", queries, keys_part, preferred_element_type=jnp.float32
    ) * HEAD_DIM ** (-0.5)
    weights = (jax.nn.silu(scores) * allowed[None] / MAXLEN).astype(jnp.bfloat16)
    attn = jnp.einsum(
        "hts,shd->thd", weights, values_part, preferred_element_type=jnp.float32
    ).reshape(tok_count, HW)
    return (layer_norm(attn) * upart.astype(jnp.float32)).astype(jnp.bfloat16)


def row_adam(rows_now, mom_now, var_now, grad, counts):
    touched = counts > 0.5
    mom_next = beta_one * mom_now + (1.0 - beta_one) * grad
    var_next = beta_two * var_now + (1.0 - beta_two) * jnp.mean(grad * grad, axis=1)
    advance = mom_next / bias_one / (jnp.sqrt(var_next / bias_two)[:, None] + adam_eps)
    rows_next = rows_now - learn_rate * advance
    return (
        jnp.where(touched[:, None], rows_next, rows_now),
        jnp.where(touched[:, None], mom_next, mom_now),
        jnp.where(touched, var_next, var_now),
    )


ROW_AXES = ("z", "y", "core")
ALL_AXES = ("z", "y", "core", "x")


def halve_sum(blocks, axis, size, dim):
    me = lax.axis_index(axis)
    lead = blocks.shape[:dim]
    bits = size.bit_length() - 1
    blocks = blocks.reshape(lead + (2,) * bits + blocks.shape[dim + 1 :])
    for bit in range(bits):
        at = dim + bits - 1 - bit
        mine = (me >> bit) & 1
        keep = lax.dynamic_index_in_dim(blocks, mine, at, keepdims=True)
        send = lax.dynamic_index_in_dim(blocks, 1 - mine, at, keepdims=True)
        pairs = [(i, i ^ (1 << bit)) for i in range(size)]
        blocks = keep + lax.ppermute(send, axis, pairs)
    return blocks.reshape(lead + blocks.shape[dim + bits :])


def double_sum(value, axis, size):
    for bit in range(size.bit_length() - 1):
        value = value + lax.ppermute(value, axis, [(i, i ^ (1 << bit)) for i in range(size)])
    return value


def reduce_weights(partial, sizes):
    width = partial.shape[1]
    n_z, n_y, n_c = sizes["z"], sizes["y"], sizes["core"]
    per_owner = partial.shape[0] // (n_z * n_y * n_c)
    blocks = partial.reshape(n_z, n_y, n_c, per_owner, width)
    blocks = halve_sum(blocks, "core", n_c, 2)
    blocks = halve_sum(blocks, "y", n_y, 1)
    blocks = halve_sum(blocks, "z", n_z, 0)
    return blocks.reshape(per_owner, width)


def local(sizes, tokens, out_grad, seq_lengths, owners, slots, w_in, w_out, emb_rows, emb_mom, emb_var):
    tok_count = tokens.shape[0]
    width = tokens.shape[1]
    allowed = allowed_mask(seq_lengths[0], tok_count)
    normed_exact, norm_back = jax.vjp(layer_norm, tokens.astype(jnp.float32))
    normed = normed_exact.astype(jnp.bfloat16)
    pre = jnp.dot(normed, w_in, preferred_element_type=jnp.float32)
    y_out, core_back = jax.vjp(lambda inner: core(inner, allowed), pre)
    y_grad = jnp.dot(out_grad, w_out, preferred_element_type=jnp.float32).astype(jnp.bfloat16)
    pre_grad_b = core_back(y_grad)[0].astype(jnp.bfloat16)
    normed_grad = lax.dot_general(
        pre_grad_b, w_in, (((1,), (1,)), ((), ())), preferred_element_type=jnp.float32
    )
    emb_grad = (norm_back(normed_grad)[0] + out_grad.astype(jnp.float32)).astype(jnp.bfloat16)
    contract = (((0,), (0,)), ((), ()))
    in_cols = w_in.shape[1]
    owner_count = 1
    for a in ROW_AXES:
        owner_count *= sizes[a]
    weight_share = reduce_weights(
        jnp.concatenate(
            [
                lax.dot_general(normed, pre_grad_b, contract, preferred_element_type=jnp.float32),
                lax.dot_general(out_grad, y_out, contract, preferred_element_type=jnp.float32),
            ],
            axis=1,
        ),
        sizes,
    )
    emb_grad, weight_share = lax.optimization_barrier((emb_grad, weight_share))
    capacity = max(2, 4 * tok_count // owner_count)
    buffer_rows = owner_count * capacity
    owner_of = owners[:, 0]
    position = jnp.arange(tok_count, dtype=jnp.int32)
    earlier = jnp.sum(
        ((owner_of[:, None] == owner_of[None, :]) & (position[None, :] < position[:, None])).astype(
            jnp.int32
        ),
        axis=1,
    )
    position_to = owner_of * capacity + earlier
    chosen = position_to[None, :] == jnp.arange(buffer_rows, dtype=jnp.int32)[:, None]
    outgoing = jnp.dot(
        chosen.astype(jnp.bfloat16), emb_grad, preferred_element_type=jnp.float32
    ).astype(jnp.bfloat16)
    outgoing = outgoing.reshape(owner_count, capacity, width)
    out_slots = (jnp.sum(jnp.where(chosen, slots[None, :] + 1, 0), axis=1) - 1).reshape(
        owner_count, capacity
    )
    slot_row = jnp.zeros((owner_count, 1, width), jnp.bfloat16)
    slot_row = slot_row.at[:, 0, :capacity].set(out_slots.astype(jnp.bfloat16))
    arrived = lax.all_to_all(
        jnp.concatenate([outgoing, slot_row], axis=1), ROW_AXES, 0, 0, tiled=True
    )
    received = arrived[:, :capacity, :].reshape(buffer_rows, width)
    got_slots = arrived[:, capacity, :capacity].astype(jnp.int32).reshape(buffer_rows)
    slot_count = emb_rows.shape[0]
    matches = got_slots[None, :] == jnp.arange(slot_count, dtype=jnp.int32)[:, None]
    grad_part = jnp.dot(matches.astype(jnp.bfloat16), received, preferred_element_type=jnp.float32)
    count_part = jnp.sum(matches.astype(jnp.float32), axis=1)
    lanes = width + 128
    both = double_sum(
        jnp.concatenate(
            [
                jnp.concatenate(
                    [grad_part, jnp.broadcast_to(count_part[:, None], (slot_count, 128))], axis=1
                ),
                weight_share.reshape(-1, lanes),
            ],
            axis=0,
        ),
        "x",
        sizes["x"],
    )
    grad_all, count_all = both[:slot_count, :width], both[:slot_count, width]
    weight_share = both[slot_count:].reshape(weight_share.shape)
    w_in_grad = weight_share[:, :in_cols]
    w_out_grad = weight_share[:, in_cols:]
    new_rows, new_mom, new_var = row_adam(emb_rows, emb_mom, emb_var, grad_all, count_all)
    return (new_rows, new_mom, new_var, w_in_grad, w_out_grad)


def solution(mesh):
    n_rows, n_dp = mesh.shape["rows"], mesh.shape["dp"]
    sizes = {"core": 2, "y": 4}
    sizes["z"] = n_rows // (sizes["core"] * sizes["y"])
    sizes["x"] = n_dp
    fine = Mesh(
        mesh.devices.reshape(sizes["z"], sizes["y"], sizes["core"], sizes["x"]), ALL_AXES
    )
    tok = P(ALL_AXES, None)
    own = P(ROW_AXES, None)
    in_specs = (tok, tok, tok, tok, P(ALL_AXES), P(), P(), own, own, P(ROW_AXES))
    out_specs = (own, own, P(ROW_AXES), own, own)
    return jax.shard_map(
        functools.partial(local, sizes), mesh=fine, in_specs=in_specs, out_specs=out_specs,
        check_vma=False,
    )
```

```python
import functools

import jax
import jax.numpy as jnp
from jax import lax
from jax.sharding import Mesh, PartitionSpec as P

HEADS = 4
HEAD_DIM = 64
HW = 256
MAXLEN = 256


norm_eps = 1e-06
beta_one = 0.9
beta_two = 0.99
learn_rate = 0.05
adam_eps = 1e-08
bias_one = 1.0 - 0.9**10
bias_two = 1.0 - 0.99**10


def layer_norm(values):
    average = jnp.mean(values, axis=-1, keepdims=True)
    centered = values - average
    spread = jnp.mean(centered * centered, axis=-1, keepdims=True)
    return centered * lax.rsqrt(spread + norm_eps)


def allowed_mask(lengths, tok_count):
    ends = jnp.cumsum(lengths)
    position = jnp.arange(tok_count, dtype=jnp.int32)
    segment = jnp.sum((position[:, None] >= ends[None, :]).astype(jnp.int32), axis=1)
    same = segment[:, None] == segment[None, :]
    causal = position[None, :] <= position[:, None]
    return (same & causal).astype(jnp.float32)


def core(pre, allowed):
    tok_count = pre.shape[0]
    proj = jax.nn.silu(pre).astype(jnp.bfloat16)
    upart, vpart, qpart, kpart = jnp.split(proj, 4, axis=1)
    queries = qpart.reshape(tok_count, HEADS, HEAD_DIM)
    keys_part = kpart.reshape(tok_count, HEADS, HEAD_DIM)
    values_part = vpart.reshape(tok_count, HEADS, HEAD_DIM)
    scores = jnp.einsum(
        "thd,shd->hts", queries, keys_part, preferred_element_type=jnp.float32
    ) * HEAD_DIM ** (-0.5)
    weights = (jax.nn.silu(scores) * allowed[None] / MAXLEN).astype(jnp.bfloat16)
    attn = jnp.einsum(
        "hts,shd->thd", weights, values_part, preferred_element_type=jnp.float32
    ).reshape(tok_count, HW)
    return (layer_norm(attn) * upart.astype(jnp.float32)).astype(jnp.bfloat16)


def row_adam(rows_now, mom_now, var_now, grad, counts):
    touched = counts > 0.5
    mom_next = beta_one * mom_now + (1.0 - beta_one) * grad
    var_next = beta_two * var_now + (1.0 - beta_two) * jnp.mean(grad * grad, axis=1)
    advance = mom_next / bias_one / (jnp.sqrt(var_next / bias_two)[:, None] + adam_eps)
    rows_next = rows_now - learn_rate * advance
    return (
        jnp.where(touched[:, None], rows_next, rows_now),
        jnp.where(touched[:, None], mom_next, mom_now),
        jnp.where(touched, var_next, var_now),
    )


ROW_AXES = ("z", "y", "core")
ALL_AXES = ("z", "y", "core", "x")


def halve_sum(blocks, axis, size, dim):
    me = lax.axis_index(axis)
    lead = blocks.shape[:dim]
    bits = size.bit_length() - 1
    blocks = blocks.reshape(lead + (2,) * bits + blocks.shape[dim + 1 :])
    for bit in range(bits):
        at = dim + bits - 1 - bit
        mine = (me >> bit) & 1
        keep = lax.dynamic_index_in_dim(blocks, mine, at, keepdims=True)
        send = lax.dynamic_index_in_dim(blocks, 1 - mine, at, keepdims=True)
        pairs = [(i, i ^ (1 << bit)) for i in range(size)]
        blocks = keep + lax.ppermute(send, axis, pairs)
    return blocks.reshape(lead + blocks.shape[dim + bits :])


def double_sum(value, axis, size):
    for bit in range(size.bit_length() - 1):
        value = value + lax.ppermute(value, axis, [(i, i ^ (1 << bit)) for i in range(size)])
    return value


def reduce_weights(partial, sizes):
    width = partial.shape[1]
    n_z, n_y, n_c = sizes["z"], sizes["y"], sizes["core"]
    per_owner = partial.shape[0] // (n_z * n_y * n_c)
    blocks = partial.reshape(n_z, n_y, n_c, per_owner, width)
    blocks = halve_sum(blocks, "core", n_c, 2)
    blocks = halve_sum(blocks, "y", n_y, 1)
    blocks = halve_sum(blocks, "z", n_z, 0)
    return blocks.reshape(per_owner, width)


def local(sizes, tokens, out_grad, seq_lengths, owners, slots, w_in, w_out, emb_rows, emb_mom, emb_var):
    tok_count = tokens.shape[0]
    width = tokens.shape[1]
    allowed = allowed_mask(seq_lengths[0], tok_count)
    normed_exact, norm_back = jax.vjp(layer_norm, tokens.astype(jnp.float32))
    normed = normed_exact.astype(jnp.bfloat16)
    pre = jnp.dot(normed, w_in, preferred_element_type=jnp.float32)
    y_out, core_back = jax.vjp(lambda inner: core(inner, allowed), pre)
    y_grad = jnp.dot(out_grad, w_out, preferred_element_type=jnp.float32).astype(jnp.bfloat16)
    pre_grad_b = core_back(y_grad)[0].astype(jnp.bfloat16)
    normed_grad = lax.dot_general(
        pre_grad_b, w_in, (((1,), (1,)), ((), ())), preferred_element_type=jnp.float32
    )
    emb_grad = (norm_back(normed_grad)[0] + out_grad.astype(jnp.float32)).astype(jnp.bfloat16)
    contract = (((0,), (0,)), ((), ()))
    in_cols = w_in.shape[1]
    owner_count = 1
    for a in ROW_AXES:
        owner_count *= sizes[a]
    weight_share = reduce_weights(
        jnp.concatenate(
            [
                lax.dot_general(normed, pre_grad_b, contract, preferred_element_type=jnp.float32),
                lax.dot_general(out_grad, y_out, contract, preferred_element_type=jnp.float32),
            ],
            axis=1,
        ),
        sizes,
    )
    capacity = max(2, 4 * tok_count // owner_count)
    buffer_rows = owner_count * capacity
    owner_of = owners[:, 0]
    position = jnp.arange(tok_count, dtype=jnp.int32)
    earlier = jnp.sum(
        ((owner_of[:, None] == owner_of[None, :]) & (position[None, :] < position[:, None])).astype(
            jnp.int32
        ),
        axis=1,
    )
    position_to = owner_of * capacity + earlier
    chosen = position_to[None, :] == jnp.arange(buffer_rows, dtype=jnp.int32)[:, None]
    outgoing = jnp.dot(
        chosen.astype(jnp.bfloat16), emb_grad, preferred_element_type=jnp.float32
    ).astype(jnp.bfloat16)
    outgoing = outgoing.reshape(owner_count, capacity, width)
    out_slots = (jnp.sum(jnp.where(chosen, slots[None, :] + 1, 0), axis=1) - 1).reshape(
        owner_count, capacity
    )
    block_rows = capacity * width // 128
    slot_row = jnp.zeros((owner_count, 1, 128), jnp.bfloat16)
    slot_row = slot_row.at[:, 0, :capacity].set(out_slots.astype(jnp.bfloat16))
    arrived = lax.all_to_all(
        jnp.concatenate([outgoing.reshape(owner_count, block_rows, 128), slot_row], axis=1),
        ROW_AXES,
        0,
        0,
        tiled=True,
    )
    arrived, weight_share = lax.optimization_barrier((arrived, weight_share))
    received = arrived[:, :block_rows, :].reshape(buffer_rows, width)
    got_slots = arrived[:, block_rows, :capacity].astype(jnp.int32).reshape(buffer_rows)
    slot_count = emb_rows.shape[0]
    matches = got_slots[None, :] == jnp.arange(slot_count, dtype=jnp.int32)[:, None]
    grad_part = jnp.dot(matches.astype(jnp.bfloat16), received, preferred_element_type=jnp.float32)
    count_part = jnp.sum(matches.astype(jnp.float32), axis=1)
    lanes = width + 128
    both = double_sum(
        jnp.concatenate(
            [
                jnp.concatenate(
                    [grad_part, jnp.broadcast_to(count_part[:, None], (slot_count, 128))], axis=1
                ),
                weight_share.reshape(-1, lanes),
            ],
            axis=0,
        ),
        "x",
        sizes["x"],
    )
    grad_all, count_all = both[:slot_count, :width], both[:slot_count, width]
    weight_share = both[slot_count:].reshape(weight_share.shape)
    w_in_grad = weight_share[:, :in_cols]
    w_out_grad = weight_share[:, in_cols:]
    new_rows, new_mom, new_var = row_adam(emb_rows, emb_mom, emb_var, grad_all, count_all)
    return (new_rows, new_mom, new_var, w_in_grad, w_out_grad)


def solution(mesh):
    n_rows, n_dp = mesh.shape["rows"], mesh.shape["dp"]
    sizes = {"core": 2, "y": 4}
    sizes["z"] = n_rows // (sizes["core"] * sizes["y"])
    sizes["x"] = n_dp
    fine = Mesh(
        mesh.devices.reshape(sizes["z"], sizes["y"], sizes["core"], sizes["x"]), ALL_AXES
    )
    tok = P(ALL_AXES, None)
    own = P(ROW_AXES, None)
    in_specs = (tok, tok, tok, tok, P(ALL_AXES), P(), P(), own, own, P(ROW_AXES))
    out_specs = (own, own, P(ROW_AXES), own, own)
    return jax.shard_map(
        functools.partial(local, sizes), mesh=fine, in_specs=in_specs, out_specs=out_specs,
        check_vma=False,
    )
```

```python
import functools

import jax
import jax.numpy as jnp
from jax import lax
from jax.sharding import Mesh, PartitionSpec as P

HEADS = 4
HEAD_DIM = 64
HW = 256
MAXLEN = 256


norm_eps = 1e-06
beta_one = 0.9
beta_two = 0.99
learn_rate = 0.05
adam_eps = 1e-08
bias_one = 1.0 - 0.9**10
bias_two = 1.0 - 0.99**10


def layer_norm(values):
    average = jnp.mean(values, axis=-1, keepdims=True)
    centered = values - average
    spread = jnp.mean(centered * centered, axis=-1, keepdims=True)
    return centered * lax.rsqrt(spread + norm_eps)


def allowed_mask(lengths, tok_count):
    ends = jnp.cumsum(lengths)
    position = jnp.arange(tok_count, dtype=jnp.int32)
    segment = jnp.sum((position[:, None] >= ends[None, :]).astype(jnp.int32), axis=1)
    same = segment[:, None] == segment[None, :]
    causal = position[None, :] <= position[:, None]
    return (same & causal).astype(jnp.float32)


def core(pre, allowed):
    tok_count = pre.shape[0]
    proj = jax.nn.silu(pre).astype(jnp.bfloat16)
    upart, vpart, qpart, kpart = jnp.split(proj, 4, axis=1)
    queries = qpart.reshape(tok_count, HEADS, HEAD_DIM)
    keys_part = kpart.reshape(tok_count, HEADS, HEAD_DIM)
    values_part = vpart.reshape(tok_count, HEADS, HEAD_DIM)
    scores = jnp.einsum(
        "thd,shd->hts", queries, keys_part, preferred_element_type=jnp.float32
    ) * HEAD_DIM ** (-0.5)
    weights = (jax.nn.silu(scores) * allowed[None] / MAXLEN).astype(jnp.bfloat16)
    attn = jnp.einsum(
        "hts,shd->thd", weights, values_part, preferred_element_type=jnp.float32
    ).reshape(tok_count, HW)
    return (layer_norm(attn) * upart.astype(jnp.float32)).astype(jnp.bfloat16)


def row_adam(rows_now, mom_now, var_now, grad, counts):
    touched = counts > 0.5
    mom_next = beta_one * mom_now + (1.0 - beta_one) * grad
    var_next = beta_two * var_now + (1.0 - beta_two) * jnp.mean(grad * grad, axis=1)
    advance = mom_next / bias_one / (jnp.sqrt(var_next / bias_two)[:, None] + adam_eps)
    rows_next = rows_now - learn_rate * advance
    return (
        jnp.where(touched[:, None], rows_next, rows_now),
        jnp.where(touched[:, None], mom_next, mom_now),
        jnp.where(touched, var_next, var_now),
    )


ROW_AXES = ("z", "y", "core")
ALL_AXES = ("z", "y", "core", "x")


def halve_sum(blocks, axis, size, dim):
    me = lax.axis_index(axis)
    lead = blocks.shape[:dim]
    bits = size.bit_length() - 1
    blocks = blocks.reshape(lead + (2,) * bits + blocks.shape[dim + 1 :])
    for bit in range(bits):
        at = dim + bits - 1 - bit
        mine = (me >> bit) & 1
        keep = lax.dynamic_index_in_dim(blocks, mine, at, keepdims=True)
        send = lax.dynamic_index_in_dim(blocks, 1 - mine, at, keepdims=True)
        pairs = [(i, i ^ (1 << bit)) for i in range(size)]
        blocks = keep + lax.ppermute(send, axis, pairs)
    return blocks.reshape(lead + blocks.shape[dim + bits :])


def double_sum(value, axis, size):
    for bit in range(size.bit_length() - 1):
        value = value + lax.ppermute(value, axis, [(i, i ^ (1 << bit)) for i in range(size)])
    return value


def reduce_weights(partial, sizes):
    width = partial.shape[1]
    n_z, n_y, n_c = sizes["z"], sizes["y"], sizes["core"]
    per_owner = partial.shape[0] // (n_z * n_y * n_c)
    blocks = partial.reshape(n_z, n_y, n_c, per_owner, width)
    blocks = halve_sum(blocks, "core", n_c, 2)
    blocks = halve_sum(blocks, "y", n_y, 1)
    blocks = halve_sum(blocks, "z", n_z, 0)
    return blocks.reshape(per_owner, width)


def local(sizes, tokens, out_grad, seq_lengths, owners, slots, w_in, w_out, emb_rows, emb_mom, emb_var):
    tok_count = tokens.shape[0]
    width = tokens.shape[1]
    allowed = allowed_mask(seq_lengths[0], tok_count)
    normed_exact, norm_back = jax.vjp(layer_norm, tokens.astype(jnp.float32))
    normed = normed_exact.astype(jnp.bfloat16)
    pre = jnp.dot(normed, w_in, preferred_element_type=jnp.float32)
    y_out, core_back = jax.vjp(lambda inner: core(inner, allowed), pre)
    y_grad = jnp.dot(out_grad, w_out, preferred_element_type=jnp.float32).astype(jnp.bfloat16)
    pre_grad_b = core_back(y_grad)[0].astype(jnp.bfloat16)
    normed_grad = lax.dot_general(
        pre_grad_b, w_in, (((1,), (1,)), ((), ())), preferred_element_type=jnp.float32
    )
    emb_grad = (norm_back(normed_grad)[0] + out_grad.astype(jnp.float32)).astype(jnp.bfloat16)
    contract = (((0,), (0,)), ((), ()))
    in_cols = w_in.shape[1]
    owner_count = 1
    for a in ROW_AXES:
        owner_count *= sizes[a]
    weight_share = reduce_weights(
        jnp.concatenate(
            [
                lax.dot_general(normed, pre_grad_b, contract, preferred_element_type=jnp.float32),
                lax.dot_general(out_grad, y_out, contract, preferred_element_type=jnp.float32),
            ],
            axis=1,
        ),
        sizes,
    )
    capacity = max(2, 4 * tok_count // owner_count)
    buffer_rows = owner_count * capacity
    owner_of = owners[:, 0]
    position = jnp.arange(tok_count, dtype=jnp.int32)
    earlier = jnp.sum(
        ((owner_of[:, None] == owner_of[None, :]) & (position[None, :] < position[:, None])).astype(
            jnp.int32
        ),
        axis=1,
    )
    position_to = owner_of * capacity + earlier
    chosen = position_to[None, :] == jnp.arange(buffer_rows, dtype=jnp.int32)[:, None]
    lane_blocks = width // 128
    outgoing = jnp.stack(
        [
            jnp.dot(
                chosen.astype(jnp.bfloat16),
                emb_grad[:, j * 128 : (j + 1) * 128],
                preferred_element_type=jnp.float32,
            )
            .astype(jnp.bfloat16)
            .reshape(owner_count, capacity, 128)
            for j in range(lane_blocks)
        ],
        axis=1,
    )
    out_slots = (jnp.sum(jnp.where(chosen, slots[None, :] + 1, 0), axis=1) - 1).reshape(
        owner_count, capacity
    )
    block_rows = capacity * width // 128
    slot_row = jnp.zeros((owner_count, 1, 128), jnp.bfloat16)
    slot_row = slot_row.at[:, 0, :capacity].set(out_slots.astype(jnp.bfloat16))
    arrived = lax.all_to_all(
        jnp.concatenate([outgoing.reshape(owner_count, block_rows, 128), slot_row], axis=1),
        ROW_AXES,
        0,
        0,
        tiled=True,
    )
    arrived, weight_share = lax.optimization_barrier((arrived, weight_share))
    received = arrived[:, :block_rows, :].reshape(owner_count, lane_blocks, capacity, 128)
    got_slots = arrived[:, block_rows, :capacity].astype(jnp.int32).reshape(buffer_rows)
    slot_count = emb_rows.shape[0]
    matches = got_slots[None, :] == jnp.arange(slot_count, dtype=jnp.int32)[:, None]
    grad_part = jnp.concatenate(
        [
            jnp.dot(
                matches.astype(jnp.bfloat16),
                received[:, j].reshape(buffer_rows, 128),
                preferred_element_type=jnp.float32,
            )
            for j in range(lane_blocks)
        ],
        axis=1,
    )
    count_part = jnp.sum(matches.astype(jnp.float32), axis=1)
    lanes = width + 128
    both = double_sum(
        jnp.concatenate(
            [
                jnp.concatenate(
                    [grad_part, jnp.broadcast_to(count_part[:, None], (slot_count, 128))], axis=1
                ),
                weight_share.reshape(-1, lanes),
            ],
            axis=0,
        ),
        "x",
        sizes["x"],
    )
    grad_all, count_all = both[:slot_count, :width], both[:slot_count, width]
    weight_share = both[slot_count:].reshape(weight_share.shape)
    w_in_grad = weight_share[:, :in_cols]
    w_out_grad = weight_share[:, in_cols:]
    new_rows, new_mom, new_var = row_adam(emb_rows, emb_mom, emb_var, grad_all, count_all)
    return (new_rows, new_mom, new_var, w_in_grad, w_out_grad)


def solution(mesh):
    n_rows, n_dp = mesh.shape["rows"], mesh.shape["dp"]
    sizes = {"core": 2, "y": 4}
    sizes["z"] = n_rows // (sizes["core"] * sizes["y"])
    sizes["x"] = n_dp
    fine = Mesh(
        mesh.devices.reshape(sizes["z"], sizes["y"], sizes["core"], sizes["x"]), ALL_AXES
    )
    tok = P(ALL_AXES, None)
    own = P(ROW_AXES, None)
    in_specs = (tok, tok, tok, tok, P(ALL_AXES), P(), P(), own, own, P(ROW_AXES))
    out_specs = (own, own, P(ROW_AXES), own, own)
    return jax.shard_map(
        functools.partial(local, sizes), mesh=fine, in_specs=in_specs, out_specs=out_specs,
        check_vma=False,
    )
```

```python
import functools

import jax
import jax.numpy as jnp
from jax import lax
from jax.sharding import Mesh, PartitionSpec as P

HEADS = 4
HEAD_DIM = 64
HW = 256
MAXLEN = 256


norm_eps = 1e-06
beta_one = 0.9
beta_two = 0.99
learn_rate = 0.05
adam_eps = 1e-08
bias_one = 1.0 - 0.9**10
bias_two = 1.0 - 0.99**10


def layer_norm(values):
    average = jnp.mean(values, axis=-1, keepdims=True)
    centered = values - average
    spread = jnp.mean(centered * centered, axis=-1, keepdims=True)
    return centered * lax.rsqrt(spread + norm_eps)


def allowed_mask(lengths, tok_count):
    ends = jnp.cumsum(lengths)
    position = jnp.arange(tok_count, dtype=jnp.int32)
    segment = jnp.sum((position[:, None] >= ends[None, :]).astype(jnp.int32), axis=1)
    same = segment[:, None] == segment[None, :]
    causal = position[None, :] <= position[:, None]
    return (same & causal).astype(jnp.float32)


def core(pre, allowed):
    tok_count = pre.shape[0]
    proj = jax.nn.silu(pre).astype(jnp.bfloat16)
    upart, vpart, qpart, kpart = jnp.split(proj, 4, axis=1)
    queries = qpart.reshape(tok_count, HEADS, HEAD_DIM)
    keys_part = kpart.reshape(tok_count, HEADS, HEAD_DIM)
    values_part = vpart.reshape(tok_count, HEADS, HEAD_DIM)
    scores = jnp.einsum(
        "thd,shd->hts", queries, keys_part, preferred_element_type=jnp.float32
    ) * HEAD_DIM ** (-0.5)
    weights = (jax.nn.silu(scores) * allowed[None] / MAXLEN).astype(jnp.bfloat16)
    attn = jnp.einsum(
        "hts,shd->thd", weights, values_part, preferred_element_type=jnp.float32
    ).reshape(tok_count, HW)
    return (layer_norm(attn) * upart.astype(jnp.float32)).astype(jnp.bfloat16)


def row_adam(rows_now, mom_now, var_now, grad, counts):
    touched = counts > 0.5
    mom_next = beta_one * mom_now + (1.0 - beta_one) * grad
    var_next = beta_two * var_now + (1.0 - beta_two) * jnp.mean(grad * grad, axis=1)
    advance = mom_next / bias_one / (jnp.sqrt(var_next / bias_two)[:, None] + adam_eps)
    rows_next = rows_now - learn_rate * advance
    return (
        jnp.where(touched[:, None], rows_next, rows_now),
        jnp.where(touched[:, None], mom_next, mom_now),
        jnp.where(touched, var_next, var_now),
    )


ROW_AXES = ("z", "y", "core")
ALL_AXES = ("z", "y", "core", "x")


def halve_sum(blocks, axis, size, dim):
    me = lax.axis_index(axis)
    lead = blocks.shape[:dim]
    bits = size.bit_length() - 1
    blocks = blocks.reshape(lead + (2,) * bits + blocks.shape[dim + 1 :])
    for bit in range(bits):
        at = dim + bits - 1 - bit
        mine = (me >> bit) & 1
        keep = lax.dynamic_index_in_dim(blocks, mine, at, keepdims=True)
        send = lax.dynamic_index_in_dim(blocks, 1 - mine, at, keepdims=True)
        pairs = [(i, i ^ (1 << bit)) for i in range(size)]
        blocks = keep + lax.ppermute(send, axis, pairs)
    return blocks.reshape(lead + blocks.shape[dim + bits :])


def double_sum(value, axis, size):
    for bit in range(size.bit_length() - 1):
        value = value + lax.ppermute(value, axis, [(i, i ^ (1 << bit)) for i in range(size)])
    return value


def reduce_weights(partial, sizes):
    width = partial.shape[1]
    n_z, n_y, n_c, n_x = sizes["z"], sizes["y"], sizes["core"], sizes["x"]
    per_owner = partial.shape[0] // (n_z * n_y * n_c)
    blocks = partial.reshape(n_z, n_y, n_c, per_owner, width)
    blocks = halve_sum(blocks, "core", n_c, 2)
    blocks = blocks.reshape(n_z, n_y, n_x, per_owner // n_x, width)
    blocks = halve_sum(blocks, "x", n_x, 2)
    piece = lax.psum_scatter(blocks.reshape(n_z, -1, 128), "z", scatter_dimension=0, tiled=True)
    piece = lax.psum_scatter(piece.reshape(n_y, -1, 128), "y", scatter_dimension=0, tiled=True)
    piece = piece.reshape(per_owner // n_x, width)
    mine = lax.axis_index("x") * (per_owner // n_x)
    return lax.dynamic_update_slice_in_dim(jnp.zeros((per_owner, width), piece.dtype), piece, mine, 0)


def local(sizes, tokens, out_grad, seq_lengths, owners, slots, w_in, w_out, emb_rows, emb_mom, emb_var):
    tok_count = tokens.shape[0]
    width = tokens.shape[1]
    allowed = allowed_mask(seq_lengths[0], tok_count)
    normed_exact, norm_back = jax.vjp(layer_norm, tokens.astype(jnp.float32))
    normed = normed_exact.astype(jnp.bfloat16)
    pre = jnp.dot(normed, w_in, preferred_element_type=jnp.float32)
    y_out, core_back = jax.vjp(lambda inner: core(inner, allowed), pre)
    y_grad = jnp.dot(out_grad, w_out, preferred_element_type=jnp.float32).astype(jnp.bfloat16)
    pre_grad_b = core_back(y_grad)[0].astype(jnp.bfloat16)
    normed_grad = lax.dot_general(
        pre_grad_b, w_in, (((1,), (1,)), ((), ())), preferred_element_type=jnp.float32
    )
    emb_grad = (norm_back(normed_grad)[0] + out_grad.astype(jnp.float32)).astype(jnp.bfloat16)
    contract = (((0,), (0,)), ((), ()))
    in_cols = w_in.shape[1]
    owner_count = 1
    for a in ROW_AXES:
        owner_count *= sizes[a]
    weight_share = reduce_weights(
        jnp.concatenate(
            [
                lax.dot_general(normed, pre_grad_b, contract, preferred_element_type=jnp.float32),
                lax.dot_general(out_grad, y_out, contract, preferred_element_type=jnp.float32),
            ],
            axis=1,
        ),
        sizes,
    )
    capacity = max(2, 4 * tok_count // owner_count)
    buffer_rows = owner_count * capacity
    owner_of = owners[:, 0]
    position = jnp.arange(tok_count, dtype=jnp.int32)
    earlier = jnp.sum(
        ((owner_of[:, None] == owner_of[None, :]) & (position[None, :] < position[:, None])).astype(
            jnp.int32
        ),
        axis=1,
    )
    position_to = owner_of * capacity + earlier
    chosen = position_to[None, :] == jnp.arange(buffer_rows, dtype=jnp.int32)[:, None]
    outgoing = jnp.dot(
        chosen.astype(jnp.bfloat16), emb_grad, preferred_element_type=jnp.float32
    ).astype(jnp.bfloat16)
    outgoing = outgoing.reshape(owner_count, capacity, width)
    out_slots = (jnp.sum(jnp.where(chosen, slots[None, :] + 1, 0), axis=1) - 1).reshape(
        owner_count, capacity
    )
    block_rows = capacity * width // 128
    slot_row = jnp.zeros((owner_count, 1, 128), jnp.bfloat16)
    slot_row = slot_row.at[:, 0, :capacity].set(out_slots.astype(jnp.bfloat16))
    arrived = lax.all_to_all(
        jnp.concatenate([outgoing.reshape(owner_count, block_rows, 128), slot_row], axis=1),
        ROW_AXES,
        0,
        0,
        tiled=True,
    )
    arrived, weight_share = lax.optimization_barrier((arrived, weight_share))
    received = arrived[:, :block_rows, :].reshape(buffer_rows, width)
    got_slots = arrived[:, block_rows, :capacity].astype(jnp.int32).reshape(buffer_rows)
    slot_count = emb_rows.shape[0]
    matches = got_slots[None, :] == jnp.arange(slot_count, dtype=jnp.int32)[:, None]
    grad_part = jnp.dot(matches.astype(jnp.bfloat16), received, preferred_element_type=jnp.float32)
    count_part = jnp.sum(matches.astype(jnp.float32), axis=1)
    lanes = width + 128
    both = double_sum(
        jnp.concatenate(
            [
                jnp.concatenate(
                    [grad_part, jnp.broadcast_to(count_part[:, None], (slot_count, 128))], axis=1
                ),
                weight_share.reshape(-1, lanes),
            ],
            axis=0,
        ),
        "x",
        sizes["x"],
    )
    grad_all, count_all = both[:slot_count, :width], both[:slot_count, width]
    weight_share = both[slot_count:].reshape(weight_share.shape)
    w_in_grad = weight_share[:, :in_cols]
    w_out_grad = weight_share[:, in_cols:]
    new_rows, new_mom, new_var = row_adam(emb_rows, emb_mom, emb_var, grad_all, count_all)
    return (new_rows, new_mom, new_var, w_in_grad, w_out_grad)


def solution(mesh):
    n_rows, n_dp = mesh.shape["rows"], mesh.shape["dp"]
    sizes = {"core": 2, "y": 4}
    sizes["z"] = n_rows // (sizes["core"] * sizes["y"])
    sizes["x"] = n_dp
    fine = Mesh(
        mesh.devices.reshape(sizes["z"], sizes["y"], sizes["core"], sizes["x"]), ALL_AXES
    )
    tok = P(ALL_AXES, None)
    own = P(ROW_AXES, None)
    in_specs = (tok, tok, tok, tok, P(ALL_AXES), P(), P(), own, own, P(ROW_AXES))
    out_specs = (own, own, P(ROW_AXES), own, own)
    return jax.shard_map(
        functools.partial(local, sizes), mesh=fine, in_specs=in_specs, out_specs=out_specs,
        check_vma=False,
    )
```

```python
import functools

import jax
import jax.numpy as jnp
from jax import lax
from jax.sharding import Mesh, PartitionSpec as P

HEADS = 4
HEAD_DIM = 64
HW = 256
MAXLEN = 256


norm_eps = 1e-06
beta_one = 0.9
beta_two = 0.99
learn_rate = 0.05
adam_eps = 1e-08
bias_one = 1.0 - 0.9**10
bias_two = 1.0 - 0.99**10


def layer_norm(values):
    average = jnp.mean(values, axis=-1, keepdims=True)
    centered = values - average
    spread = jnp.mean(centered * centered, axis=-1, keepdims=True)
    return centered * lax.rsqrt(spread + norm_eps)


def allowed_mask(lengths, tok_count):
    ends = jnp.cumsum(lengths)
    position = jnp.arange(tok_count, dtype=jnp.int32)
    segment = jnp.sum((position[:, None] >= ends[None, :]).astype(jnp.int32), axis=1)
    same = segment[:, None] == segment[None, :]
    causal = position[None, :] <= position[:, None]
    return (same & causal).astype(jnp.float32)


def core(pre, allowed):
    tok_count = pre.shape[0]
    proj = jax.nn.silu(pre).astype(jnp.bfloat16)
    upart, vpart, qpart, kpart = jnp.split(proj, 4, axis=1)
    queries = qpart.reshape(tok_count, HEADS, HEAD_DIM)
    keys_part = kpart.reshape(tok_count, HEADS, HEAD_DIM)
    values_part = vpart.reshape(tok_count, HEADS, HEAD_DIM)
    scores = jnp.einsum(
        "thd,shd->hts", queries, keys_part, preferred_element_type=jnp.float32
    ) * HEAD_DIM ** (-0.5)
    weights = (jax.nn.silu(scores) * allowed[None] / MAXLEN).astype(jnp.bfloat16)
    attn = jnp.einsum(
        "hts,shd->thd", weights, values_part, preferred_element_type=jnp.float32
    ).reshape(tok_count, HW)
    return (layer_norm(attn) * upart.astype(jnp.float32)).astype(jnp.bfloat16)


def row_adam(rows_now, mom_now, var_now, grad, counts):
    touched = counts > 0.5
    mom_next = beta_one * mom_now + (1.0 - beta_one) * grad
    var_next = beta_two * var_now + (1.0 - beta_two) * jnp.mean(grad * grad, axis=1)
    advance = mom_next / bias_one / (jnp.sqrt(var_next / bias_two)[:, None] + adam_eps)
    rows_next = rows_now - learn_rate * advance
    return (
        jnp.where(touched[:, None], rows_next, rows_now),
        jnp.where(touched[:, None], mom_next, mom_now),
        jnp.where(touched, var_next, var_now),
    )


ROW_AXES = ("z", "y", "core")
ALL_AXES = ("z", "y", "core", "x")


def halve_sum(blocks, axis, size, dim):
    me = lax.axis_index(axis)
    lead = blocks.shape[:dim]
    bits = size.bit_length() - 1
    blocks = blocks.reshape(lead + (2,) * bits + blocks.shape[dim + 1 :])
    for bit in range(bits):
        at = dim + bits - 1 - bit
        mine = (me >> bit) & 1
        keep = lax.dynamic_index_in_dim(blocks, mine, at, keepdims=True)
        send = lax.dynamic_index_in_dim(blocks, 1 - mine, at, keepdims=True)
        pairs = [(i, i ^ (1 << bit)) for i in range(size)]
        blocks = keep + lax.ppermute(send, axis, pairs)
    return blocks.reshape(lead + blocks.shape[dim + bits :])


def double_sum(value, axis, size):
    for bit in range(size.bit_length() - 1):
        value = value + lax.ppermute(value, axis, [(i, i ^ (1 << bit)) for i in range(size)])
    return value


def reduce_weights(partial, sizes):
    width = partial.shape[1]
    n_z, n_y, n_c, n_x = sizes["z"], sizes["y"], sizes["core"], sizes["x"]
    per_owner = partial.shape[0] // (n_z * n_y * n_c)
    blocks = partial.reshape(n_z, n_y, n_c, per_owner, width)
    blocks = halve_sum(blocks, "core", n_c, 2)
    blocks = blocks.reshape(n_z, n_y, n_x, per_owner // n_x, width)
    blocks = halve_sum(blocks, "x", n_x, 2)
    blocks = halve_sum(blocks, "y", n_y, 1)
    piece = halve_sum(blocks, "z", n_z, 0)
    mine = lax.axis_index("x") * (per_owner // n_x)
    return lax.dynamic_update_slice_in_dim(jnp.zeros((per_owner, width), piece.dtype), piece, mine, 0)


def local(sizes, tokens, out_grad, seq_lengths, owners, slots, w_in, w_out, emb_rows, emb_mom, emb_var):
    tok_count = tokens.shape[0]
    width = tokens.shape[1]
    allowed = allowed_mask(seq_lengths[0], tok_count)
    normed_exact, norm_back = jax.vjp(layer_norm, tokens.astype(jnp.float32))
    normed = normed_exact.astype(jnp.bfloat16)
    pre = jnp.dot(normed, w_in, preferred_element_type=jnp.float32)
    y_out, core_back = jax.vjp(lambda inner: core(inner, allowed), pre)
    y_grad = jnp.dot(out_grad, w_out, preferred_element_type=jnp.float32).astype(jnp.bfloat16)
    pre_grad_b = core_back(y_grad)[0].astype(jnp.bfloat16)
    normed_grad = lax.dot_general(
        pre_grad_b, w_in, (((1,), (1,)), ((), ())), preferred_element_type=jnp.float32
    )
    emb_grad = (norm_back(normed_grad)[0] + out_grad.astype(jnp.float32)).astype(jnp.bfloat16)
    contract = (((0,), (0,)), ((), ()))
    in_cols = w_in.shape[1]
    owner_count = 1
    for a in ROW_AXES:
        owner_count *= sizes[a]
    weight_share = reduce_weights(
        jnp.concatenate(
            [
                lax.dot_general(normed, pre_grad_b, contract, preferred_element_type=jnp.float32),
                lax.dot_general(out_grad, y_out, contract, preferred_element_type=jnp.float32),
            ],
            axis=1,
        ),
        sizes,
    )
    capacity = max(2, 4 * tok_count // owner_count)
    buffer_rows = owner_count * capacity
    owner_of = owners[:, 0]
    position = jnp.arange(tok_count, dtype=jnp.int32)
    earlier = jnp.sum(
        ((owner_of[:, None] == owner_of[None, :]) & (position[None, :] < position[:, None])).astype(
            jnp.int32
        ),
        axis=1,
    )
    position_to = owner_of * capacity + earlier
    chosen = position_to[None, :] == jnp.arange(buffer_rows, dtype=jnp.int32)[:, None]
    outgoing = jnp.dot(
        chosen.astype(jnp.bfloat16), emb_grad, preferred_element_type=jnp.float32
    ).astype(jnp.bfloat16)
    outgoing = outgoing.reshape(owner_count, capacity, width)
    out_slots = (jnp.sum(jnp.where(chosen, slots[None, :] + 1, 0), axis=1) - 1).reshape(
        owner_count, capacity
    )
    block_rows = capacity * width // 128
    slot_row = jnp.zeros((owner_count, 1, 128), jnp.bfloat16)
    slot_row = slot_row.at[:, 0, :capacity].set(out_slots.astype(jnp.bfloat16))
    arrived = lax.all_to_all(
        jnp.concatenate([outgoing.reshape(owner_count, block_rows, 128), slot_row], axis=1),
        ROW_AXES,
        0,
        0,
        tiled=True,
    )
    arrived, weight_share = lax.optimization_barrier((arrived, weight_share))
    received = arrived[:, :block_rows, :].reshape(buffer_rows, width)
    got_slots = arrived[:, block_rows, :capacity].astype(jnp.int32).reshape(buffer_rows)
    slot_count = emb_rows.shape[0]
    matches = got_slots[None, :] == jnp.arange(slot_count, dtype=jnp.int32)[:, None]
    grad_part = jnp.dot(matches.astype(jnp.bfloat16), received, preferred_element_type=jnp.float32)
    count_part = jnp.sum(matches.astype(jnp.float32), axis=1)
    lanes = width + 128
    both = double_sum(
        jnp.concatenate(
            [
                jnp.concatenate(
                    [grad_part, jnp.broadcast_to(count_part[:, None], (slot_count, 128))], axis=1
                ),
                weight_share.reshape(-1, lanes),
            ],
            axis=0,
        ),
        "x",
        sizes["x"],
    )
    grad_all, count_all = both[:slot_count, :width], both[:slot_count, width]
    weight_share = both[slot_count:].reshape(weight_share.shape)
    w_in_grad = weight_share[:, :in_cols]
    w_out_grad = weight_share[:, in_cols:]
    new_rows, new_mom, new_var = row_adam(emb_rows, emb_mom, emb_var, grad_all, count_all)
    return (new_rows, new_mom, new_var, w_in_grad, w_out_grad)


def solution(mesh):
    n_rows, n_dp = mesh.shape["rows"], mesh.shape["dp"]
    sizes = {"core": 2, "y": 4}
    sizes["z"] = n_rows // (sizes["core"] * sizes["y"])
    sizes["x"] = n_dp
    fine = Mesh(
        mesh.devices.reshape(sizes["z"], sizes["y"], sizes["core"], sizes["x"]), ALL_AXES
    )
    tok = P(ALL_AXES, None)
    own = P(ROW_AXES, None)
    in_specs = (tok, tok, tok, tok, P(ALL_AXES), P(), P(), own, own, P(ROW_AXES))
    out_specs = (own, own, P(ROW_AXES), own, own)
    return jax.shard_map(
        functools.partial(local, sizes), mesh=fine, in_specs=in_specs, out_specs=out_specs,
        check_vma=False,
    )
```

```python
import functools

import jax
import jax.numpy as jnp
from jax import lax
from jax.sharding import Mesh, PartitionSpec as P

HEADS = 4
HEAD_DIM = 64
HW = 256
MAXLEN = 256


norm_eps = 1e-06
beta_one = 0.9
beta_two = 0.99
learn_rate = 0.05
adam_eps = 1e-08
bias_one = 1.0 - 0.9**10
bias_two = 1.0 - 0.99**10


def layer_norm(values):
    average = jnp.mean(values, axis=-1, keepdims=True)
    centered = values - average
    spread = jnp.mean(centered * centered, axis=-1, keepdims=True)
    return centered * lax.rsqrt(spread + norm_eps)


def allowed_mask(lengths, tok_count):
    ends = jnp.cumsum(lengths)
    position = jnp.arange(tok_count, dtype=jnp.int32)
    segment = jnp.sum((position[:, None] >= ends[None, :]).astype(jnp.int32), axis=1)
    same = segment[:, None] == segment[None, :]
    causal = position[None, :] <= position[:, None]
    return (same & causal).astype(jnp.float32)


def core(pre, allowed):
    tok_count = pre.shape[0]
    proj = jax.nn.silu(pre).astype(jnp.bfloat16)
    upart, vpart, qpart, kpart = jnp.split(proj, 4, axis=1)
    queries = qpart.reshape(tok_count, HEADS, HEAD_DIM)
    keys_part = kpart.reshape(tok_count, HEADS, HEAD_DIM)
    values_part = vpart.reshape(tok_count, HEADS, HEAD_DIM)
    scores = jnp.einsum(
        "thd,shd->hts", queries, keys_part, preferred_element_type=jnp.float32
    ) * HEAD_DIM ** (-0.5)
    weights = (jax.nn.silu(scores) * allowed[None] / MAXLEN).astype(jnp.bfloat16)
    attn = jnp.einsum(
        "hts,shd->thd", weights, values_part, preferred_element_type=jnp.float32
    ).reshape(tok_count, HW)
    return (layer_norm(attn) * upart.astype(jnp.float32)).astype(jnp.bfloat16)


def row_adam(rows_now, mom_now, var_now, grad, counts):
    touched = counts > 0.5
    mom_next = beta_one * mom_now + (1.0 - beta_one) * grad
    var_next = beta_two * var_now + (1.0 - beta_two) * jnp.mean(grad * grad, axis=1)
    advance = mom_next / bias_one / (jnp.sqrt(var_next / bias_two)[:, None] + adam_eps)
    rows_next = rows_now - learn_rate * advance
    return (
        jnp.where(touched[:, None], rows_next, rows_now),
        jnp.where(touched[:, None], mom_next, mom_now),
        jnp.where(touched, var_next, var_now),
    )


ROW_AXES = ("z", "y", "core")
ALL_AXES = ("z", "y", "core", "x")


def halve_sum(blocks, axis, size, dim):
    me = lax.axis_index(axis)
    lead = blocks.shape[:dim]
    bits = size.bit_length() - 1
    blocks = blocks.reshape(lead + (2,) * bits + blocks.shape[dim + 1 :])
    for bit in range(bits):
        at = dim + bits - 1 - bit
        mine = (me >> bit) & 1
        keep = lax.dynamic_index_in_dim(blocks, mine, at, keepdims=True)
        send = lax.dynamic_index_in_dim(blocks, 1 - mine, at, keepdims=True)
        pairs = [(i, i ^ (1 << bit)) for i in range(size)]
        blocks = keep + lax.ppermute(send, axis, pairs)
    return blocks.reshape(lead + blocks.shape[dim + bits :])


def double_sum(value, axis, size):
    for bit in range(size.bit_length() - 1):
        value = value + lax.ppermute(value, axis, [(i, i ^ (1 << bit)) for i in range(size)])
    return value


def reduce_weights(partial, sizes):
    width = partial.shape[1]
    n_z, n_y, n_c, n_x = sizes["z"], sizes["y"], sizes["core"], sizes["x"]
    per_owner = partial.shape[0] // (n_z * n_y * n_c)
    blocks = partial.reshape(n_z, n_y, n_c, per_owner, width)
    blocks = halve_sum(blocks, "core", n_c, 2)
    blocks = blocks.reshape(n_z, n_y, n_x, per_owner // n_x, width)
    blocks = halve_sum(blocks, "x", n_x, 2)
    blocks = halve_sum(blocks, "y", n_y, 1)
    piece = halve_sum(blocks, "z", n_z, 0)
    mine = lax.axis_index("x") * (per_owner // n_x)
    return lax.dynamic_update_slice_in_dim(jnp.zeros((per_owner, width), piece.dtype), piece, mine, 0)


def local(sizes, tokens, out_grad, seq_lengths, owners, slots, w_in, w_out, emb_rows, emb_mom, emb_var):
    tok_count = tokens.shape[0]
    width = tokens.shape[1]
    allowed = allowed_mask(seq_lengths[0], tok_count)
    owner_count = 1
    for a in ROW_AXES:
        owner_count *= sizes[a]
    capacity = max(2, 4 * tok_count // owner_count)
    buffer_rows = owner_count * capacity
    owner_of = owners[:, 0]
    position = jnp.arange(tok_count, dtype=jnp.int32)
    earlier = jnp.sum(
        ((owner_of[:, None] == owner_of[None, :]) & (position[None, :] < position[:, None])).astype(
            jnp.int32
        ),
        axis=1,
    )
    position_to = owner_of * capacity + earlier
    chosen = position_to[None, :] == jnp.arange(buffer_rows, dtype=jnp.int32)[:, None]
    out_slots = (jnp.sum(jnp.where(chosen, slots[None, :] + 1, 0), axis=1) - 1).reshape(
        owner_count, capacity
    )
    got_slots = lax.all_to_all(out_slots, ROW_AXES, 0, 0, tiled=True).reshape(buffer_rows)
    got_slots, tokens = lax.optimization_barrier((got_slots, tokens))
    normed_exact, norm_back = jax.vjp(layer_norm, tokens.astype(jnp.float32))
    normed = normed_exact.astype(jnp.bfloat16)
    pre = jnp.dot(normed, w_in, preferred_element_type=jnp.float32)
    y_out, core_back = jax.vjp(lambda inner: core(inner, allowed), pre)
    y_grad = jnp.dot(out_grad, w_out, preferred_element_type=jnp.float32).astype(jnp.bfloat16)
    pre_grad_b = core_back(y_grad)[0].astype(jnp.bfloat16)
    normed_grad = lax.dot_general(
        pre_grad_b, w_in, (((1,), (1,)), ((), ())), preferred_element_type=jnp.float32
    )
    emb_grad = (norm_back(normed_grad)[0] + out_grad.astype(jnp.float32)).astype(jnp.bfloat16)
    contract = (((0,), (0,)), ((), ()))
    in_cols = w_in.shape[1]
    weight_share = reduce_weights(
        jnp.concatenate(
            [
                lax.dot_general(normed, pre_grad_b, contract, preferred_element_type=jnp.float32),
                lax.dot_general(out_grad, y_out, contract, preferred_element_type=jnp.float32),
            ],
            axis=1,
        ),
        sizes,
    )
    outgoing = jnp.dot(
        chosen.astype(jnp.bfloat16), emb_grad, preferred_element_type=jnp.float32
    ).astype(jnp.bfloat16)
    outgoing = outgoing.reshape(owner_count, capacity, width)
    arrived = lax.all_to_all(outgoing, ROW_AXES, 0, 0, tiled=True)
    arrived, weight_share = lax.optimization_barrier((arrived, weight_share))
    received = arrived.reshape(buffer_rows, width)
    slot_count = emb_rows.shape[0]
    matches = got_slots[None, :] == jnp.arange(slot_count, dtype=jnp.int32)[:, None]
    grad_part = jnp.dot(matches.astype(jnp.bfloat16), received, preferred_element_type=jnp.float32)
    count_part = jnp.sum(matches.astype(jnp.float32), axis=1)
    lanes = width + 128
    both = double_sum(
        jnp.concatenate(
            [
                jnp.concatenate(
                    [grad_part, jnp.broadcast_to(count_part[:, None], (slot_count, 128))], axis=1
                ),
                weight_share.reshape(-1, lanes),
            ],
            axis=0,
        ),
        "x",
        sizes["x"],
    )
    grad_all, count_all = both[:slot_count, :width], both[:slot_count, width]
    weight_share = both[slot_count:].reshape(weight_share.shape)
    w_in_grad = weight_share[:, :in_cols]
    w_out_grad = weight_share[:, in_cols:]
    new_rows, new_mom, new_var = row_adam(emb_rows, emb_mom, emb_var, grad_all, count_all)
    return (new_rows, new_mom, new_var, w_in_grad, w_out_grad)


def solution(mesh):
    n_rows, n_dp = mesh.shape["rows"], mesh.shape["dp"]
    sizes = {"core": 2, "y": 4}
    sizes["z"] = n_rows // (sizes["core"] * sizes["y"])
    sizes["x"] = n_dp
    fine = Mesh(
        mesh.devices.reshape(sizes["z"], sizes["y"], sizes["core"], sizes["x"]), ALL_AXES
    )
    tok = P(ALL_AXES, None)
    own = P(ROW_AXES, None)
    in_specs = (tok, tok, tok, tok, P(ALL_AXES), P(), P(), own, own, P(ROW_AXES))
    out_specs = (own, own, P(ROW_AXES), own, own)
    return jax.shard_map(
        functools.partial(local, sizes), mesh=fine, in_specs=in_specs, out_specs=out_specs,
        check_vma=False,
    )
```

```python
import functools

import jax
import jax.numpy as jnp
from jax import lax
from jax.sharding import Mesh, PartitionSpec as P

HEADS = 4
HEAD_DIM = 64
HW = 256
MAXLEN = 256


norm_eps = 1e-06
beta_one = 0.9
beta_two = 0.99
learn_rate = 0.05
adam_eps = 1e-08
bias_one = 1.0 - 0.9**10
bias_two = 1.0 - 0.99**10


def layer_norm(values):
    average = jnp.mean(values, axis=-1, keepdims=True)
    centered = values - average
    spread = jnp.mean(centered * centered, axis=-1, keepdims=True)
    return centered * lax.rsqrt(spread + norm_eps)


def allowed_mask(lengths, tok_count):
    ends = jnp.cumsum(lengths)
    position = jnp.arange(tok_count, dtype=jnp.int32)
    segment = jnp.sum((position[:, None] >= ends[None, :]).astype(jnp.int32), axis=1)
    same = segment[:, None] == segment[None, :]
    causal = position[None, :] <= position[:, None]
    return (same & causal).astype(jnp.float32)


def core(pre, allowed):
    tok_count = pre.shape[0]
    proj = jax.nn.silu(pre).astype(jnp.bfloat16)
    upart, vpart, qpart, kpart = jnp.split(proj, 4, axis=1)
    queries = qpart.reshape(tok_count, HEADS, HEAD_DIM)
    keys_part = kpart.reshape(tok_count, HEADS, HEAD_DIM)
    values_part = vpart.reshape(tok_count, HEADS, HEAD_DIM)
    scores = jnp.einsum(
        "thd,shd->hts", queries, keys_part, preferred_element_type=jnp.float32
    ) * HEAD_DIM ** (-0.5)
    weights = (jax.nn.silu(scores) * allowed[None] / MAXLEN).astype(jnp.bfloat16)
    attn = jnp.einsum(
        "hts,shd->thd", weights, values_part, preferred_element_type=jnp.float32
    ).reshape(tok_count, HW)
    return (layer_norm(attn) * upart.astype(jnp.float32)).astype(jnp.bfloat16)


def row_adam(rows_now, mom_now, var_now, grad, counts):
    touched = counts > 0.5
    mom_next = beta_one * mom_now + (1.0 - beta_one) * grad
    var_next = beta_two * var_now + (1.0 - beta_two) * jnp.mean(grad * grad, axis=1)
    advance = mom_next / bias_one / (jnp.sqrt(var_next / bias_two)[:, None] + adam_eps)
    rows_next = rows_now - learn_rate * advance
    return (
        jnp.where(touched[:, None], rows_next, rows_now),
        jnp.where(touched[:, None], mom_next, mom_now),
        jnp.where(touched, var_next, var_now),
    )


ROW_AXES = ("z", "y", "core")
ALL_AXES = ("z", "y", "core", "x")


def halve_sum(blocks, axis, size, dim):
    me = lax.axis_index(axis)
    lead = blocks.shape[:dim]
    bits = size.bit_length() - 1
    blocks = blocks.reshape(lead + (2,) * bits + blocks.shape[dim + 1 :])
    for bit in range(bits):
        at = dim + bits - 1 - bit
        mine = (me >> bit) & 1
        keep = lax.dynamic_index_in_dim(blocks, mine, at, keepdims=True)
        send = lax.dynamic_index_in_dim(blocks, 1 - mine, at, keepdims=True)
        pairs = [(i, i ^ (1 << bit)) for i in range(size)]
        blocks = keep + lax.ppermute(send, axis, pairs)
    return blocks.reshape(lead + blocks.shape[dim + bits :])


def double_sum(value, axis, size):
    for bit in range(size.bit_length() - 1):
        value = value + lax.ppermute(value, axis, [(i, i ^ (1 << bit)) for i in range(size)])
    return value


def reduce_weights(partial, sizes):
    width = partial.shape[1]
    n_z, n_y, n_c, n_x = sizes["z"], sizes["y"], sizes["core"], sizes["x"]
    per_owner = partial.shape[0] // (n_z * n_y * n_c)
    blocks = partial.reshape(n_z, n_y, n_c, per_owner, width)
    blocks = halve_sum(blocks, "core", n_c, 2)
    blocks = blocks.reshape(n_z, n_y, n_x, per_owner // n_x, width)
    blocks = halve_sum(blocks, "x", n_x, 2)
    return blocks


def finish_weights(blocks, sizes):
    n_z, n_y, n_x = sizes["z"], sizes["y"], sizes["x"]
    per_owner, width = blocks.shape[2] * n_x, blocks.shape[3]
    blocks = halve_sum(blocks, "y", n_y, 1)
    piece = halve_sum(blocks, "z", n_z, 0)
    mine = lax.axis_index("x") * (per_owner // n_x)
    return lax.dynamic_update_slice_in_dim(jnp.zeros((per_owner, width), piece.dtype), piece, mine, 0)


def local(sizes, tokens, out_grad, seq_lengths, owners, slots, w_in, w_out, emb_rows, emb_mom, emb_var):
    tok_count = tokens.shape[0]
    width = tokens.shape[1]
    allowed = allowed_mask(seq_lengths[0], tok_count)
    owner_count = 1
    for a in ROW_AXES:
        owner_count *= sizes[a]
    capacity = max(2, 4 * tok_count // owner_count)
    buffer_rows = owner_count * capacity
    owner_of = owners[:, 0]
    position = jnp.arange(tok_count, dtype=jnp.int32)
    earlier = jnp.sum(
        ((owner_of[:, None] == owner_of[None, :]) & (position[None, :] < position[:, None])).astype(
            jnp.int32
        ),
        axis=1,
    )
    position_to = owner_of * capacity + earlier
    chosen = position_to[None, :] == jnp.arange(buffer_rows, dtype=jnp.int32)[:, None]
    out_slots = (jnp.sum(jnp.where(chosen, slots[None, :] + 1, 0), axis=1) - 1).reshape(
        owner_count, capacity
    )
    got_slots = lax.all_to_all(out_slots, ROW_AXES, 0, 0, tiled=True).reshape(buffer_rows)
    got_slots, tokens = lax.optimization_barrier((got_slots, tokens))
    normed_exact, norm_back = jax.vjp(layer_norm, tokens.astype(jnp.float32))
    normed = normed_exact.astype(jnp.bfloat16)
    pre = jnp.dot(normed, w_in, preferred_element_type=jnp.float32)
    y_out, core_back = jax.vjp(lambda inner: core(inner, allowed), pre)
    y_grad = jnp.dot(out_grad, w_out, preferred_element_type=jnp.float32).astype(jnp.bfloat16)
    pre_grad_b = core_back(y_grad)[0].astype(jnp.bfloat16)
    normed_grad = lax.dot_general(
        pre_grad_b, w_in, (((1,), (1,)), ((), ())), preferred_element_type=jnp.float32
    )
    emb_grad = (norm_back(normed_grad)[0] + out_grad.astype(jnp.float32)).astype(jnp.bfloat16)
    contract = (((0,), (0,)), ((), ()))
    in_cols = w_in.shape[1]
    weight_share = reduce_weights(
        jnp.concatenate(
            [
                lax.dot_general(normed, pre_grad_b, contract, preferred_element_type=jnp.float32),
                lax.dot_general(out_grad, y_out, contract, preferred_element_type=jnp.float32),
            ],
            axis=1,
        ),
        sizes,
    )
    outgoing = jnp.dot(
        chosen.astype(jnp.bfloat16), emb_grad, preferred_element_type=jnp.float32
    ).astype(jnp.bfloat16)
    outgoing = outgoing.reshape(owner_count, capacity, width)
    outgoing, weight_share = lax.optimization_barrier((outgoing, weight_share))
    arrived = lax.all_to_all(outgoing, ROW_AXES, 0, 0, tiled=True)
    weight_share = finish_weights(weight_share, sizes)
    arrived, weight_share = lax.optimization_barrier((arrived, weight_share))
    received = arrived.reshape(buffer_rows, width)
    slot_count = emb_rows.shape[0]
    matches = got_slots[None, :] == jnp.arange(slot_count, dtype=jnp.int32)[:, None]
    grad_part = jnp.dot(matches.astype(jnp.bfloat16), received, preferred_element_type=jnp.float32)
    count_part = jnp.sum(matches.astype(jnp.float32), axis=1)
    lanes = width + 128
    both = double_sum(
        jnp.concatenate(
            [
                jnp.concatenate(
                    [grad_part, jnp.broadcast_to(count_part[:, None], (slot_count, 128))], axis=1
                ),
                weight_share.reshape(-1, lanes),
            ],
            axis=0,
        ),
        "x",
        sizes["x"],
    )
    grad_all, count_all = both[:slot_count, :width], both[:slot_count, width]
    weight_share = both[slot_count:].reshape(weight_share.shape)
    w_in_grad = weight_share[:, :in_cols]
    w_out_grad = weight_share[:, in_cols:]
    new_rows, new_mom, new_var = row_adam(emb_rows, emb_mom, emb_var, grad_all, count_all)
    return (new_rows, new_mom, new_var, w_in_grad, w_out_grad)


def solution(mesh):
    n_rows, n_dp = mesh.shape["rows"], mesh.shape["dp"]
    sizes = {"core": 2, "y": 4}
    sizes["z"] = n_rows // (sizes["core"] * sizes["y"])
    sizes["x"] = n_dp
    fine = Mesh(
        mesh.devices.reshape(sizes["z"], sizes["y"], sizes["core"], sizes["x"]), ALL_AXES
    )
    tok = P(ALL_AXES, None)
    own = P(ROW_AXES, None)
    in_specs = (tok, tok, tok, tok, P(ALL_AXES), P(), P(), own, own, P(ROW_AXES))
    out_specs = (own, own, P(ROW_AXES), own, own)
    return jax.shard_map(
        functools.partial(local, sizes), mesh=fine, in_specs=in_specs, out_specs=out_specs,
        check_vma=False,
    )
```

```python
import functools

import jax
import jax.numpy as jnp
from jax import lax
from jax.sharding import Mesh, PartitionSpec as P

HEADS = 4
HEAD_DIM = 64
HW = 256
MAXLEN = 256


norm_eps = 1e-06
beta_one = 0.9
beta_two = 0.99
learn_rate = 0.05
adam_eps = 1e-08
bias_one = 1.0 - 0.9**10
bias_two = 1.0 - 0.99**10


def layer_norm(values):
    average = jnp.mean(values, axis=-1, keepdims=True)
    centered = values - average
    spread = jnp.mean(centered * centered, axis=-1, keepdims=True)
    return centered * lax.rsqrt(spread + norm_eps)


def allowed_mask(lengths, tok_count):
    ends = jnp.cumsum(lengths)
    position = jnp.arange(tok_count, dtype=jnp.int32)
    segment = jnp.sum((position[:, None] >= ends[None, :]).astype(jnp.int32), axis=1)
    same = segment[:, None] == segment[None, :]
    causal = position[None, :] <= position[:, None]
    return (same & causal).astype(jnp.float32)


def core(pre, allowed):
    tok_count = pre.shape[0]
    proj = jax.nn.silu(pre).astype(jnp.bfloat16)
    upart, vpart, qpart, kpart = jnp.split(proj, 4, axis=1)
    queries = qpart.reshape(tok_count, HEADS, HEAD_DIM)
    keys_part = kpart.reshape(tok_count, HEADS, HEAD_DIM)
    values_part = vpart.reshape(tok_count, HEADS, HEAD_DIM)
    scores = jnp.einsum(
        "thd,shd->hts", queries, keys_part, preferred_element_type=jnp.float32
    ) * HEAD_DIM ** (-0.5)
    weights = (jax.nn.silu(scores) * allowed[None] / MAXLEN).astype(jnp.bfloat16)
    attn = jnp.einsum(
        "hts,shd->thd", weights, values_part, preferred_element_type=jnp.float32
    ).reshape(tok_count, HW)
    return (layer_norm(attn) * upart.astype(jnp.float32)).astype(jnp.bfloat16)


def row_adam(rows_now, mom_now, var_now, grad, counts):
    touched = counts > 0.5
    mom_next = beta_one * mom_now + (1.0 - beta_one) * grad
    var_next = beta_two * var_now + (1.0 - beta_two) * jnp.mean(grad * grad, axis=1)
    advance = mom_next / bias_one / (jnp.sqrt(var_next / bias_two)[:, None] + adam_eps)
    rows_next = rows_now - learn_rate * advance
    return (
        jnp.where(touched[:, None], rows_next, rows_now),
        jnp.where(touched[:, None], mom_next, mom_now),
        jnp.where(touched, var_next, var_now),
    )


ROW_AXES = ("z", "y", "core")
ALL_AXES = ("z", "y", "core", "x")


def halve_sum(blocks, axis, size, dim):
    me = lax.axis_index(axis)
    lead = blocks.shape[:dim]
    bits = size.bit_length() - 1
    blocks = blocks.reshape(lead + (2,) * bits + blocks.shape[dim + 1 :])
    for bit in range(bits):
        at = dim + bits - 1 - bit
        mine = (me >> bit) & 1
        keep = lax.dynamic_index_in_dim(blocks, mine, at, keepdims=True)
        send = lax.dynamic_index_in_dim(blocks, 1 - mine, at, keepdims=True)
        pairs = [(i, i ^ (1 << bit)) for i in range(size)]
        blocks = keep + lax.ppermute(send, axis, pairs)
    return blocks.reshape(lead + blocks.shape[dim + bits :])


def double_sum(value, axis, size):
    for bit in range(size.bit_length() - 1):
        value = value + lax.ppermute(value, axis, [(i, i ^ (1 << bit)) for i in range(size)])
    return value


def reduce_weights(partial, sizes):
    width = partial.shape[1]
    n_z, n_y, n_c, n_x = sizes["z"], sizes["y"], sizes["core"], sizes["x"]
    per_owner = partial.shape[0] // (n_z * n_y * n_c)
    blocks = partial.reshape(n_z, n_y, n_c, per_owner, width)
    blocks = halve_sum(blocks, "core", n_c, 2)
    blocks = blocks.reshape(n_z, n_y, n_x, per_owner // n_x, width)
    blocks = halve_sum(blocks, "x", n_x, 2)
    blocks = halve_sum(blocks, "y", n_y, 1)
    piece = halve_sum(blocks, "z", n_z, 0)
    mine = lax.axis_index("x") * (per_owner // n_x)
    return lax.dynamic_update_slice_in_dim(jnp.zeros((per_owner, width), piece.dtype), piece, mine, 0)


def local(sizes, tokens, out_grad, seq_lengths, owners, slots, w_in, w_out, emb_rows, emb_mom, emb_var):
    tok_count = tokens.shape[0]
    width = tokens.shape[1]
    allowed = allowed_mask(seq_lengths[0], tok_count)
    normed_exact, norm_back = jax.vjp(layer_norm, tokens.astype(jnp.float32))
    normed = normed_exact.astype(jnp.bfloat16)
    pre = jnp.dot(normed, w_in, preferred_element_type=jnp.float32)
    y_out, core_back = jax.vjp(lambda inner: core(inner, allowed), pre)
    y_grad = jnp.dot(out_grad, w_out, preferred_element_type=jnp.float32).astype(jnp.bfloat16)
    pre_grad_b = core_back(y_grad)[0].astype(jnp.bfloat16)
    normed_grad = lax.dot_general(
        pre_grad_b, w_in, (((1,), (1,)), ((), ())), preferred_element_type=jnp.float32
    )
    emb_grad = (norm_back(normed_grad)[0] + out_grad.astype(jnp.float32)).astype(jnp.bfloat16)
    contract = (((0,), (0,)), ((), ()))
    in_cols = w_in.shape[1]
    owner_count = 1
    for a in ROW_AXES:
        owner_count *= sizes[a]
    weight_share = reduce_weights(
        jnp.concatenate(
            [
                lax.dot_general(normed, pre_grad_b, contract, preferred_element_type=jnp.float32),
                lax.dot_general(out_grad, y_out, contract, preferred_element_type=jnp.float32),
            ],
            axis=1,
        ),
        sizes,
    )
    capacity = max(2, 4 * tok_count // owner_count)
    buffer_rows = owner_count * capacity
    owner_of = owners[:, 0]
    position = jnp.arange(tok_count, dtype=jnp.int32)
    earlier = jnp.sum(
        ((owner_of[:, None] == owner_of[None, :]) & (position[None, :] < position[:, None])).astype(
            jnp.int32
        ),
        axis=1,
    )
    position_to = owner_of * capacity + earlier
    chosen = position_to[None, :] == jnp.arange(buffer_rows, dtype=jnp.int32)[:, None]
    outgoing = jnp.dot(
        chosen.astype(jnp.bfloat16), emb_grad, preferred_element_type=jnp.float32
    ).astype(jnp.bfloat16)
    outgoing = outgoing.reshape(owner_count, capacity, width)
    out_slots = (jnp.sum(jnp.where(chosen, slots[None, :] + 1, 0), axis=1) - 1).reshape(
        owner_count, capacity
    )
    block_rows = capacity * width // 128
    slot_row = jnp.zeros((owner_count, 1, 128), jnp.bfloat16)
    slot_row = slot_row.at[:, 0, :capacity].set(out_slots.astype(jnp.bfloat16))
    arrived = lax.all_to_all(
        jnp.concatenate([outgoing.reshape(owner_count, block_rows, 128), slot_row], axis=1),
        ROW_AXES,
        0,
        0,
        tiled=True,
    )
    arrived, weight_share = lax.optimization_barrier((arrived, weight_share))
    lane_blocks = width // 128
    received = arrived[:, :block_rows, :].reshape(owner_count, capacity, lane_blocks, 128)
    got_slots = arrived[:, block_rows, :capacity].astype(jnp.int32).reshape(buffer_rows)
    slot_count = emb_rows.shape[0]
    matches = got_slots[None, :] == jnp.arange(slot_count, dtype=jnp.int32)[:, None]
    grad_part = jnp.concatenate(
        [
            jnp.dot(
                matches.astype(jnp.bfloat16),
                received[:, :, j, :].reshape(buffer_rows, 128),
                preferred_element_type=jnp.float32,
            )
            for j in range(lane_blocks)
        ],
        axis=1,
    )
    count_part = jnp.sum(matches.astype(jnp.float32), axis=1)
    lanes = width + 128
    both = double_sum(
        jnp.concatenate(
            [
                jnp.concatenate(
                    [grad_part, jnp.broadcast_to(count_part[:, None], (slot_count, 128))], axis=1
                ),
                weight_share.reshape(-1, lanes),
            ],
            axis=0,
        ),
        "x",
        sizes["x"],
    )
    grad_all, count_all = both[:slot_count, :width], both[:slot_count, width]
    weight_share = both[slot_count:].reshape(weight_share.shape)
    w_in_grad = weight_share[:, :in_cols]
    w_out_grad = weight_share[:, in_cols:]
    new_rows, new_mom, new_var = row_adam(emb_rows, emb_mom, emb_var, grad_all, count_all)
    return (new_rows, new_mom, new_var, w_in_grad, w_out_grad)


def solution(mesh):
    n_rows, n_dp = mesh.shape["rows"], mesh.shape["dp"]
    sizes = {"core": 2, "y": 4}
    sizes["z"] = n_rows // (sizes["core"] * sizes["y"])
    sizes["x"] = n_dp
    fine = Mesh(
        mesh.devices.reshape(sizes["z"], sizes["y"], sizes["core"], sizes["x"]), ALL_AXES
    )
    tok = P(ALL_AXES, None)
    own = P(ROW_AXES, None)
    in_specs = (tok, tok, tok, tok, P(ALL_AXES), P(), P(), own, own, P(ROW_AXES))
    out_specs = (own, own, P(ROW_AXES), own, own)
    return jax.shard_map(
        functools.partial(local, sizes), mesh=fine, in_specs=in_specs, out_specs=out_specs,
        check_vma=False,
    )
```

```python
import functools

import jax
import jax.numpy as jnp
from jax import lax
from jax.sharding import Mesh, PartitionSpec as P

HEADS = 4
HEAD_DIM = 64
HW = 256
MAXLEN = 256


norm_eps = 1e-06
beta_one = 0.9
beta_two = 0.99
learn_rate = 0.05
adam_eps = 1e-08
bias_one = 1.0 - 0.9**10
bias_two = 1.0 - 0.99**10


def layer_norm(values):
    average = jnp.mean(values, axis=-1, keepdims=True)
    centered = values - average
    spread = jnp.mean(centered * centered, axis=-1, keepdims=True)
    return centered * lax.rsqrt(spread + norm_eps)


def allowed_mask(lengths, tok_count):
    ends = jnp.cumsum(lengths)
    position = jnp.arange(tok_count, dtype=jnp.int32)
    segment = jnp.sum((position[:, None] >= ends[None, :]).astype(jnp.int32), axis=1)
    same = segment[:, None] == segment[None, :]
    causal = position[None, :] <= position[:, None]
    return (same & causal).astype(jnp.float32)


def core(pre, allowed):
    tok_count = pre.shape[0]
    proj = jax.nn.silu(pre).astype(jnp.bfloat16)
    upart, vpart, qpart, kpart = jnp.split(proj, 4, axis=1)
    queries = qpart.reshape(tok_count, HEADS, HEAD_DIM)
    keys_part = kpart.reshape(tok_count, HEADS, HEAD_DIM)
    values_part = vpart.reshape(tok_count, HEADS, HEAD_DIM)
    scores = jnp.einsum(
        "thd,shd->hts", queries, keys_part, preferred_element_type=jnp.float32
    ) * HEAD_DIM ** (-0.5)
    weights = (jax.nn.silu(scores) * allowed[None] / MAXLEN).astype(jnp.bfloat16)
    attn = jnp.einsum(
        "hts,shd->thd", weights, values_part, preferred_element_type=jnp.float32
    ).reshape(tok_count, HW)
    return (layer_norm(attn) * upart.astype(jnp.float32)).astype(jnp.bfloat16)


def row_adam(rows_now, mom_now, var_now, grad, counts):
    touched = counts > 0.5
    mom_next = beta_one * mom_now + (1.0 - beta_one) * grad
    var_next = beta_two * var_now + (1.0 - beta_two) * jnp.mean(grad * grad, axis=1)
    advance = mom_next / bias_one / (jnp.sqrt(var_next / bias_two)[:, None] + adam_eps)
    rows_next = rows_now - learn_rate * advance
    return (
        jnp.where(touched[:, None], rows_next, rows_now),
        jnp.where(touched[:, None], mom_next, mom_now),
        jnp.where(touched, var_next, var_now),
    )


ROW_AXES = ("z", "y", "core")
ALL_AXES = ("z", "y", "core", "x")


def halve_sum(blocks, axis, size, dim):
    me = lax.axis_index(axis)
    lead = blocks.shape[:dim]
    bits = size.bit_length() - 1
    blocks = blocks.reshape(lead + (2,) * bits + blocks.shape[dim + 1 :])
    for bit in range(bits):
        at = dim + bits - 1 - bit
        mine = (me >> bit) & 1
        keep = lax.dynamic_index_in_dim(blocks, mine, at, keepdims=True)
        send = lax.dynamic_index_in_dim(blocks, 1 - mine, at, keepdims=True)
        pairs = [(i, i ^ (1 << bit)) for i in range(size)]
        blocks = keep + lax.ppermute(send, axis, pairs)
    return blocks.reshape(lead + blocks.shape[dim + bits :])


def double_sum(value, axis, size):
    for bit in range(size.bit_length() - 1):
        value = value + lax.ppermute(value, axis, [(i, i ^ (1 << bit)) for i in range(size)])
    return value


def reduce_weights(partial, sizes):
    width = partial.shape[1]
    n_z, n_y, n_c, n_x = sizes["z"], sizes["y"], sizes["core"], sizes["x"]
    per_owner = partial.shape[0] // (n_z * n_y * n_c)
    blocks = partial.reshape(n_z, n_y, n_c, per_owner, width)
    blocks = halve_sum(blocks, "core", n_c, 2)
    blocks = blocks.reshape(n_z, n_y, n_x, per_owner // n_x, width)
    blocks = halve_sum(blocks, "x", n_x, 2)
    blocks = halve_sum(blocks, "y", n_y, 1)
    piece = halve_sum(blocks, "z", n_z, 0)
    mine = lax.axis_index("x") * (per_owner // n_x)
    return lax.dynamic_update_slice_in_dim(jnp.zeros((per_owner, width), piece.dtype), piece, mine, 0)


def local(sizes, tokens, out_grad, seq_lengths, owners, slots, w_in, w_out, emb_rows, emb_mom, emb_var):
    tok_count = tokens.shape[0]
    width = tokens.shape[1]
    allowed = allowed_mask(seq_lengths[0], tok_count)
    normed_exact, norm_back = jax.vjp(layer_norm, tokens.astype(jnp.float32))
    normed = normed_exact.astype(jnp.bfloat16)
    pre = jnp.dot(normed, w_in, preferred_element_type=jnp.float32)
    y_out, core_back = jax.vjp(lambda inner: core(inner, allowed), pre)
    y_grad = jnp.dot(out_grad, w_out, preferred_element_type=jnp.float32).astype(jnp.bfloat16)
    pre_grad_b = core_back(y_grad)[0].astype(jnp.bfloat16)
    normed_grad = lax.dot_general(
        pre_grad_b, w_in, (((1,), (1,)), ((), ())), preferred_element_type=jnp.float32
    )
    emb_grad = (norm_back(normed_grad)[0] + out_grad.astype(jnp.float32)).astype(jnp.bfloat16)
    contract = (((0,), (0,)), ((), ()))
    in_cols = w_in.shape[1]
    owner_count = 1
    for a in ROW_AXES:
        owner_count *= sizes[a]
    weight_share = reduce_weights(
        jnp.concatenate(
            [
                lax.dot_general(normed, pre_grad_b, contract, preferred_element_type=jnp.float32),
                lax.dot_general(out_grad, y_out, contract, preferred_element_type=jnp.float32),
            ],
            axis=1,
        ),
        sizes,
    )
    capacity = max(2, 4 * tok_count // owner_count)
    buffer_rows = owner_count * capacity
    owner_of = owners[:, 0]
    position = jnp.arange(tok_count, dtype=jnp.int32)
    earlier = jnp.sum(
        ((owner_of[:, None] == owner_of[None, :]) & (position[None, :] < position[:, None])).astype(
            jnp.int32
        ),
        axis=1,
    )
    position_to = owner_of * capacity + earlier
    chosen = position_to[None, :] == jnp.arange(buffer_rows, dtype=jnp.int32)[:, None]
    outgoing = jnp.dot(
        chosen.astype(jnp.bfloat16), emb_grad, preferred_element_type=jnp.float32
    ).astype(jnp.bfloat16)
    outgoing = outgoing.reshape(owner_count, capacity, width)
    out_slots = (jnp.sum(jnp.where(chosen, slots[None, :] + 1, 0), axis=1) - 1).reshape(
        owner_count, capacity
    )
    block_rows = capacity * width // 128
    slot_row = jnp.zeros((owner_count, 1, 128), jnp.bfloat16)
    slot_row = slot_row.at[:, 0, :capacity].set(out_slots.astype(jnp.bfloat16))
    arrived = lax.all_to_all(
        jnp.concatenate([outgoing.reshape(owner_count, block_rows, 128), slot_row], axis=1),
        ROW_AXES,
        0,
        0,
        tiled=True,
    )
    arrived, weight_share = lax.optimization_barrier((arrived, weight_share))
    lane_blocks = width // 128
    received = arrived[:, :block_rows, :].reshape(owner_count, capacity, lane_blocks, 128)
    got_slots = arrived[:, block_rows, :capacity].astype(jnp.int32).reshape(buffer_rows)
    slot_count = emb_rows.shape[0]
    matches = got_slots[None, :] == jnp.arange(slot_count, dtype=jnp.int32)[:, None]
    grad_part = jnp.concatenate(
        [
            jnp.dot(
                matches.astype(jnp.bfloat16),
                received[:, :, j, :].reshape(buffer_rows, 128),
                preferred_element_type=jnp.float32,
            )
            for j in range(lane_blocks)
        ],
        axis=1,
    )
    count_part = jnp.sum(matches.astype(jnp.float32), axis=1)
    weight_rows = weight_share.size // width
    count_rows = slot_count // width + 1
    counts = jnp.zeros((count_rows * width,), jnp.float32).at[:slot_count].set(count_part)
    both = double_sum(
        jnp.concatenate(
            [grad_part, weight_share.reshape(weight_rows, width), counts.reshape(count_rows, width)],
            axis=0,
        ),
        "x",
        sizes["x"],
    )
    grad_all = both[:slot_count]
    weight_share = both[slot_count : slot_count + weight_rows].reshape(weight_share.shape)
    count_all = both[slot_count + weight_rows :].reshape(-1)[:slot_count]
    w_in_grad = weight_share[:, :in_cols]
    w_out_grad = weight_share[:, in_cols:]
    new_rows, new_mom, new_var = row_adam(emb_rows, emb_mom, emb_var, grad_all, count_all)
    return (new_rows, new_mom, new_var, w_in_grad, w_out_grad)


def solution(mesh):
    n_rows, n_dp = mesh.shape["rows"], mesh.shape["dp"]
    sizes = {"core": 2, "y": 4}
    sizes["z"] = n_rows // (sizes["core"] * sizes["y"])
    sizes["x"] = n_dp
    fine = Mesh(
        mesh.devices.reshape(sizes["z"], sizes["y"], sizes["core"], sizes["x"]), ALL_AXES
    )
    tok = P(ALL_AXES, None)
    own = P(ROW_AXES, None)
    in_specs = (tok, tok, tok, tok, P(ALL_AXES), P(), P(), own, own, P(ROW_AXES))
    out_specs = (own, own, P(ROW_AXES), own, own)
    return jax.shard_map(
        functools.partial(local, sizes), mesh=fine, in_specs=in_specs, out_specs=out_specs,
        check_vma=False,
    )
```

```python
import functools

import jax
import jax.numpy as jnp
from jax import lax
from jax.sharding import Mesh, PartitionSpec as P

HEADS = 4
HEAD_DIM = 64
HW = 256
MAXLEN = 256


norm_eps = 1e-06
beta_one = 0.9
beta_two = 0.99
learn_rate = 0.05
adam_eps = 1e-08
bias_one = 1.0 - 0.9**10
bias_two = 1.0 - 0.99**10


def layer_norm(values):
    average = jnp.mean(values, axis=-1, keepdims=True)
    centered = values - average
    spread = jnp.mean(centered * centered, axis=-1, keepdims=True)
    return centered * lax.rsqrt(spread + norm_eps)


def allowed_mask(lengths, tok_count):
    ends = jnp.cumsum(lengths)
    position = jnp.arange(tok_count, dtype=jnp.int32)
    segment = jnp.sum((position[:, None] >= ends[None, :]).astype(jnp.int32), axis=1)
    same = segment[:, None] == segment[None, :]
    causal = position[None, :] <= position[:, None]
    return (same & causal).astype(jnp.float32)


def core(pre, allowed):
    tok_count = pre.shape[0]
    proj = jax.nn.silu(pre).astype(jnp.bfloat16)
    upart, vpart, qpart, kpart = jnp.split(proj, 4, axis=1)
    queries = qpart.reshape(tok_count, HEADS, HEAD_DIM)
    keys_part = kpart.reshape(tok_count, HEADS, HEAD_DIM)
    values_part = vpart.reshape(tok_count, HEADS, HEAD_DIM)
    scores = jnp.einsum(
        "thd,shd->hts", queries, keys_part, preferred_element_type=jnp.float32
    ) * HEAD_DIM ** (-0.5)
    weights = (jax.nn.silu(scores) * allowed[None] / MAXLEN).astype(jnp.bfloat16)
    attn = jnp.einsum(
        "hts,shd->thd", weights, values_part, preferred_element_type=jnp.float32
    ).reshape(tok_count, HW)
    return (layer_norm(attn) * upart.astype(jnp.float32)).astype(jnp.bfloat16)


def row_adam(rows_now, mom_now, var_now, grad, counts):
    touched = counts > 0.5
    mom_next = beta_one * mom_now + (1.0 - beta_one) * grad
    var_next = beta_two * var_now + (1.0 - beta_two) * jnp.mean(grad * grad, axis=1)
    advance = mom_next / bias_one / (jnp.sqrt(var_next / bias_two)[:, None] + adam_eps)
    rows_next = rows_now - learn_rate * advance
    return (
        jnp.where(touched[:, None], rows_next, rows_now),
        jnp.where(touched[:, None], mom_next, mom_now),
        jnp.where(touched, var_next, var_now),
    )


ROW_AXES = ("z", "y", "core")
ALL_AXES = ("z", "y", "core", "x")


def halve_sum(blocks, axis, size, dim):
    me = lax.axis_index(axis)
    lead = blocks.shape[:dim]
    bits = size.bit_length() - 1
    blocks = blocks.reshape(lead + (2,) * bits + blocks.shape[dim + 1 :])
    for bit in range(bits):
        at = dim + bits - 1 - bit
        mine = (me >> bit) & 1
        keep = lax.dynamic_index_in_dim(blocks, mine, at, keepdims=True)
        send = lax.dynamic_index_in_dim(blocks, 1 - mine, at, keepdims=True)
        pairs = [(i, i ^ (1 << bit)) for i in range(size)]
        blocks = keep + lax.ppermute(send, axis, pairs)
    return blocks.reshape(lead + blocks.shape[dim + bits :])


def double_sum(value, axis, size):
    for bit in range(size.bit_length() - 1):
        value = value + lax.ppermute(value, axis, [(i, i ^ (1 << bit)) for i in range(size)])
    return value


def reduce_weights(partial, sizes):
    width = partial.shape[1]
    n_z, n_y, n_c, n_x = sizes["z"], sizes["y"], sizes["core"], sizes["x"]
    per_owner = partial.shape[0] // (n_z * n_y * n_c)
    blocks = partial.reshape(n_z, n_y, n_c, per_owner, width)
    blocks = halve_sum(blocks, "core", n_c, 2)
    blocks = blocks.reshape(n_z, n_y, n_x, per_owner // n_x, width)
    blocks = halve_sum(blocks, "x", n_x, 2)
    blocks = halve_sum(blocks, "y", n_y, 1)
    piece = halve_sum(blocks, "z", n_z, 0)
    mine = lax.axis_index("x") * (per_owner // n_x)
    return lax.dynamic_update_slice_in_dim(jnp.zeros((per_owner, width), piece.dtype), piece, mine, 0)


def local(sizes, tokens, out_grad, seq_lengths, owners, slots, w_in, w_out, emb_rows, emb_mom, emb_var):
    tok_count = tokens.shape[0]
    width = tokens.shape[1]
    allowed = allowed_mask(seq_lengths[0], tok_count)
    normed_exact, norm_back = jax.vjp(layer_norm, tokens.astype(jnp.float32))
    normed = normed_exact.astype(jnp.bfloat16)
    pre = jnp.dot(normed, w_in, preferred_element_type=jnp.float32)
    y_out, core_back = jax.vjp(lambda inner: core(inner, allowed), pre)
    y_grad = jnp.dot(out_grad, w_out, preferred_element_type=jnp.float32).astype(jnp.bfloat16)
    pre_grad_b = core_back(y_grad)[0].astype(jnp.bfloat16)
    normed_grad = lax.dot_general(
        pre_grad_b, w_in, (((1,), (1,)), ((), ())), preferred_element_type=jnp.float32
    )
    emb_grad = (norm_back(normed_grad)[0] + out_grad.astype(jnp.float32)).astype(jnp.bfloat16)
    contract = (((0,), (0,)), ((), ()))
    in_cols = w_in.shape[1]
    owner_count = 1
    for a in ROW_AXES:
        owner_count *= sizes[a]
    weight_share = reduce_weights(
        jnp.concatenate(
            [
                lax.dot_general(normed, pre_grad_b, contract, preferred_element_type=jnp.float32),
                lax.dot_general(out_grad, y_out, contract, preferred_element_type=jnp.float32),
            ],
            axis=1,
        ),
        sizes,
    )
    capacity = max(2, 4 * tok_count // owner_count)
    buffer_rows = owner_count * capacity
    owner_of = owners[:, 0]
    position = jnp.arange(tok_count, dtype=jnp.int32)
    earlier = jnp.sum(
        ((owner_of[:, None] == owner_of[None, :]) & (position[None, :] < position[:, None])).astype(
            jnp.int32
        ),
        axis=1,
    )
    position_to = owner_of * capacity + earlier
    chosen = position_to[None, :] == jnp.arange(buffer_rows, dtype=jnp.int32)[:, None]
    outgoing = jnp.stack(
        [
            jnp.dot(
                chosen.astype(jnp.bfloat16),
                emb_grad[:, j * 128 : (j + 1) * 128],
                preferred_element_type=jnp.float32,
            )
            .astype(jnp.bfloat16)
            .reshape(owner_count, capacity, 128)
            for j in range(width // 128)
        ],
        axis=2,
    )
    out_slots = (jnp.sum(jnp.where(chosen, slots[None, :] + 1, 0), axis=1) - 1).reshape(
        owner_count, capacity
    )
    block_rows = capacity * width // 128
    slot_row = jnp.zeros((owner_count, 1, 128), jnp.bfloat16)
    slot_row = slot_row.at[:, 0, :capacity].set(out_slots.astype(jnp.bfloat16))
    arrived = lax.all_to_all(
        jnp.concatenate([outgoing.reshape(owner_count, block_rows, 128), slot_row], axis=1),
        ROW_AXES,
        0,
        0,
        tiled=True,
    )
    arrived, weight_share = lax.optimization_barrier((arrived, weight_share))
    lane_blocks = width // 128
    received = arrived[:, :block_rows, :].reshape(owner_count, capacity, lane_blocks, 128)
    got_slots = arrived[:, block_rows, :capacity].astype(jnp.int32).reshape(buffer_rows)
    slot_count = emb_rows.shape[0]
    matches = got_slots[None, :] == jnp.arange(slot_count, dtype=jnp.int32)[:, None]
    grad_part = jnp.concatenate(
        [
            jnp.dot(
                matches.astype(jnp.bfloat16),
                received[:, :, j, :].reshape(buffer_rows, 128),
                preferred_element_type=jnp.float32,
            )
            for j in range(lane_blocks)
        ],
        axis=1,
    )
    count_part = jnp.sum(matches.astype(jnp.float32), axis=1)
    lanes = width + 128
    both = double_sum(
        jnp.concatenate(
            [
                jnp.concatenate(
                    [grad_part, jnp.broadcast_to(count_part[:, None], (slot_count, 128))], axis=1
                ),
                weight_share.reshape(-1, lanes),
            ],
            axis=0,
        ),
        "x",
        sizes["x"],
    )
    grad_all, count_all = both[:slot_count, :width], both[:slot_count, width]
    weight_share = both[slot_count:].reshape(weight_share.shape)
    w_in_grad = weight_share[:, :in_cols]
    w_out_grad = weight_share[:, in_cols:]
    new_rows, new_mom, new_var = row_adam(emb_rows, emb_mom, emb_var, grad_all, count_all)
    return (new_rows, new_mom, new_var, w_in_grad, w_out_grad)


def solution(mesh):
    n_rows, n_dp = mesh.shape["rows"], mesh.shape["dp"]
    sizes = {"core": 2, "y": 4}
    sizes["z"] = n_rows // (sizes["core"] * sizes["y"])
    sizes["x"] = n_dp
    fine = Mesh(
        mesh.devices.reshape(sizes["z"], sizes["y"], sizes["core"], sizes["x"]), ALL_AXES
    )
    tok = P(ALL_AXES, None)
    own = P(ROW_AXES, None)
    in_specs = (tok, tok, tok, tok, P(ALL_AXES), P(), P(), own, own, P(ROW_AXES))
    out_specs = (own, own, P(ROW_AXES), own, own)
    return jax.shard_map(
        functools.partial(local, sizes), mesh=fine, in_specs=in_specs, out_specs=out_specs,
        check_vma=False,
    )
```

```python
import functools

import jax
import jax.numpy as jnp
from jax import lax
from jax.sharding import Mesh, PartitionSpec as P

HEADS = 4
HEAD_DIM = 64
HW = 256
MAXLEN = 256


norm_eps = 1e-06
beta_one = 0.9
beta_two = 0.99
learn_rate = 0.05
adam_eps = 1e-08
bias_one = 1.0 - 0.9**10
bias_two = 1.0 - 0.99**10


def layer_norm(values):
    average = jnp.mean(values, axis=-1, keepdims=True)
    centered = values - average
    spread = jnp.mean(centered * centered, axis=-1, keepdims=True)
    return centered * lax.rsqrt(spread + norm_eps)


def allowed_mask(lengths, tok_count):
    ends = jnp.cumsum(lengths)
    position = jnp.arange(tok_count, dtype=jnp.int32)
    segment = jnp.sum((position[:, None] >= ends[None, :]).astype(jnp.int32), axis=1)
    same = segment[:, None] == segment[None, :]
    causal = position[None, :] <= position[:, None]
    return (same & causal).astype(jnp.float32)


def core(pre, allowed):
    tok_count = pre.shape[0]
    proj = jax.nn.silu(pre).astype(jnp.bfloat16)
    upart, vpart, qpart, kpart = jnp.split(proj, 4, axis=1)
    queries = qpart.reshape(tok_count, HEADS, HEAD_DIM)
    keys_part = kpart.reshape(tok_count, HEADS, HEAD_DIM)
    values_part = vpart.reshape(tok_count, HEADS, HEAD_DIM)
    scores = jnp.einsum(
        "thd,shd->hts", queries, keys_part, preferred_element_type=jnp.float32
    ) * HEAD_DIM ** (-0.5)
    weights = (jax.nn.silu(scores) * allowed[None] / MAXLEN).astype(jnp.bfloat16)
    attn = jnp.einsum(
        "hts,shd->thd", weights, values_part, preferred_element_type=jnp.float32
    ).reshape(tok_count, HW)
    return (layer_norm(attn) * upart.astype(jnp.float32)).astype(jnp.bfloat16)


def row_adam(rows_now, mom_now, var_now, grad, counts):
    touched = counts > 0.5
    mom_next = beta_one * mom_now + (1.0 - beta_one) * grad
    var_next = beta_two * var_now + (1.0 - beta_two) * jnp.mean(grad * grad, axis=1)
    advance = mom_next / bias_one / (jnp.sqrt(var_next / bias_two)[:, None] + adam_eps)
    rows_next = rows_now - learn_rate * advance
    return (
        jnp.where(touched[:, None], rows_next, rows_now),
        jnp.where(touched[:, None], mom_next, mom_now),
        jnp.where(touched, var_next, var_now),
    )


ROW_AXES = ("z", "y", "core")
ALL_AXES = ("z", "y", "core", "x")


def halve_sum(blocks, axis, size, dim):
    me = lax.axis_index(axis)
    lead = blocks.shape[:dim]
    bits = size.bit_length() - 1
    blocks = blocks.reshape(lead + (2,) * bits + blocks.shape[dim + 1 :])
    for bit in range(bits):
        at = dim + bits - 1 - bit
        mine = (me >> bit) & 1
        keep = lax.dynamic_index_in_dim(blocks, mine, at, keepdims=True)
        send = lax.dynamic_index_in_dim(blocks, 1 - mine, at, keepdims=True)
        pairs = [(i, i ^ (1 << bit)) for i in range(size)]
        blocks = keep + lax.ppermute(send, axis, pairs)
    return blocks.reshape(lead + blocks.shape[dim + bits :])


def double_sum(value, axis, size):
    for bit in range(size.bit_length() - 1):
        value = value + lax.ppermute(value, axis, [(i, i ^ (1 << bit)) for i in range(size)])
    return value


def reduce_weights(partial, sizes):
    width = partial.shape[1]
    n_z, n_y, n_c, n_x = sizes["z"], sizes["y"], sizes["core"], sizes["x"]
    per_owner = partial.shape[0] // (n_z * n_y * n_c)
    blocks = partial.reshape(n_z, n_y, n_c, per_owner, width)
    blocks = halve_sum(blocks, "core", n_c, 2)
    blocks = halve_sum(blocks, "y", n_y, 1)
    return halve_sum(blocks, "z", n_z, 0).reshape(per_owner, width)


def local(sizes, tokens, out_grad, seq_lengths, owners, slots, w_in, w_out, emb_rows, emb_mom, emb_var):
    tok_count = tokens.shape[0]
    width = tokens.shape[1]
    allowed = allowed_mask(seq_lengths[0], tok_count)
    normed_exact, norm_back = jax.vjp(layer_norm, tokens.astype(jnp.float32))
    normed = normed_exact.astype(jnp.bfloat16)
    pre = jnp.dot(normed, w_in, preferred_element_type=jnp.float32)
    y_out, core_back = jax.vjp(lambda inner: core(inner, allowed), pre)
    y_grad = jnp.dot(out_grad, w_out, preferred_element_type=jnp.float32).astype(jnp.bfloat16)
    pre_grad_b = core_back(y_grad)[0].astype(jnp.bfloat16)
    normed_grad = lax.dot_general(
        pre_grad_b, w_in, (((1,), (1,)), ((), ())), preferred_element_type=jnp.float32
    )
    emb_grad = (norm_back(normed_grad)[0] + out_grad.astype(jnp.float32)).astype(jnp.bfloat16)
    contract = (((0,), (0,)), ((), ()))
    in_cols = w_in.shape[1]
    owner_count = 1
    for a in ROW_AXES:
        owner_count *= sizes[a]
    weight_share = reduce_weights(
        jnp.concatenate(
            [
                lax.dot_general(normed, pre_grad_b, contract, preferred_element_type=jnp.float32),
                lax.dot_general(out_grad, y_out, contract, preferred_element_type=jnp.float32),
            ],
            axis=1,
        ),
        sizes,
    )
    capacity = max(2, 4 * tok_count // owner_count)
    buffer_rows = owner_count * capacity
    owner_of = owners[:, 0]
    position = jnp.arange(tok_count, dtype=jnp.int32)
    earlier = jnp.sum(
        ((owner_of[:, None] == owner_of[None, :]) & (position[None, :] < position[:, None])).astype(
            jnp.int32
        ),
        axis=1,
    )
    position_to = owner_of * capacity + earlier
    chosen = position_to[None, :] == jnp.arange(buffer_rows, dtype=jnp.int32)[:, None]
    outgoing = jnp.stack(
        [
            jnp.dot(
                chosen.astype(jnp.bfloat16),
                emb_grad[:, j * 128 : (j + 1) * 128],
                preferred_element_type=jnp.float32,
            )
            .astype(jnp.bfloat16)
            .reshape(owner_count, capacity, 128)
            for j in range(width // 128)
        ],
        axis=2,
    )
    out_slots = (jnp.sum(jnp.where(chosen, slots[None, :] + 1, 0), axis=1) - 1).reshape(
        owner_count, capacity
    )
    block_rows = capacity * width // 128
    slot_row = jnp.zeros((owner_count, 1, 128), jnp.bfloat16)
    slot_row = slot_row.at[:, 0, :capacity].set(out_slots.astype(jnp.bfloat16))
    arrived = lax.all_to_all(
        jnp.concatenate([outgoing.reshape(owner_count, block_rows, 128), slot_row], axis=1),
        ROW_AXES,
        0,
        0,
        tiled=True,
    )
    arrived, weight_share = lax.optimization_barrier((arrived, weight_share))
    lane_blocks = width // 128
    received = arrived[:, :block_rows, :].reshape(owner_count, capacity, lane_blocks, 128)
    got_slots = arrived[:, block_rows, :capacity].astype(jnp.int32).reshape(buffer_rows)
    slot_count = emb_rows.shape[0]
    matches = got_slots[None, :] == jnp.arange(slot_count, dtype=jnp.int32)[:, None]
    grad_part = jnp.concatenate(
        [
            jnp.dot(
                matches.astype(jnp.bfloat16),
                received[:, :, j, :].reshape(buffer_rows, 128),
                preferred_element_type=jnp.float32,
            )
            for j in range(lane_blocks)
        ],
        axis=1,
    )
    count_part = jnp.sum(matches.astype(jnp.float32), axis=1)
    lanes = width + 128
    both = double_sum(
        jnp.concatenate(
            [
                jnp.concatenate(
                    [grad_part, jnp.broadcast_to(count_part[:, None], (slot_count, 128))], axis=1
                ),
                weight_share.reshape(-1, lanes),
            ],
            axis=0,
        ),
        "x",
        sizes["x"],
    )
    grad_all, count_all = both[:slot_count, :width], both[:slot_count, width]
    weight_share = both[slot_count:].reshape(weight_share.shape)
    w_in_grad = weight_share[:, :in_cols]
    w_out_grad = weight_share[:, in_cols:]
    new_rows, new_mom, new_var = row_adam(emb_rows, emb_mom, emb_var, grad_all, count_all)
    return (new_rows, new_mom, new_var, w_in_grad, w_out_grad)


def solution(mesh):
    n_rows, n_dp = mesh.shape["rows"], mesh.shape["dp"]
    sizes = {"core": 2, "y": 4}
    sizes["z"] = n_rows // (sizes["core"] * sizes["y"])
    sizes["x"] = n_dp
    fine = Mesh(
        mesh.devices.reshape(sizes["z"], sizes["y"], sizes["core"], sizes["x"]), ALL_AXES
    )
    tok = P(ALL_AXES, None)
    own = P(ROW_AXES, None)
    in_specs = (tok, tok, tok, tok, P(ALL_AXES), P(), P(), own, own, P(ROW_AXES))
    out_specs = (own, own, P(ROW_AXES), own, own)
    return jax.shard_map(
        functools.partial(local, sizes), mesh=fine, in_specs=in_specs, out_specs=out_specs,
        check_vma=False,
    )
```
